128 devices in a mesh: cp: 16 (over z, x), grp: 8 (over y, core).
Axes of the slice: x: 4, y: 4, z: 4, core: 2. Of those that a mesh axis runs over, the one named last changes fastest.
Arguments:
- queries: bfloat16 [32768, 8192], P(('cp', 'grp')), may hold values from -60 to 60
- keys: bfloat16 [32768, 1024], P(('cp', 'grp')), may hold values from -4 to 4
- values: bfloat16 [32768, 1024], P(('cp', 'grp')), may hold values from -6 to 6
- doc_lengths: int32 [16, 3], P('cp'), may hold values from 1 to 1536, 2048 in all within a row
- send_tile: int32 [128, 32], P(('cp', 'grp')), may hold values from 0 to 16, as said below
- take_slot: int32 [128, 16], P(('cp', 'grp')), may hold values from 0 to 31, as said below
Outputs:
- attended: bfloat16 [32768, 8192], P(('cp', 'grp'))
The draws below stay inside these ranges and needn't reach their ends.
Inputs may be any that keep to these rules, and one draw needn't show every extreme that they name: `send_tile`: entry c2 * 2 + s of row d = c * 8 + g names the arrival tile (0 to 15) that device (c, g) sends in slot s to device (c2, g), and 16 marks an empty slot. Every tile of a device is sent exactly once; each device sends 2 tiles to each of exactly 8 peers and none to the others. `take_slot`: row d2 lists, for each owner tile of device d2, the received slot c * 2 + s (slot s of the tiles sent by device (c, g) of the same g) that fills it; every filled send slot fills exactly one owner tile, so each device receives from exactly 8 peers.
All inputs are finite; a program needn't handle non-finite values.
Results may differ from the reference program's by a relative error of at most 0.0037.
Values may be sent and summed in bfloat16 or wider, within the bound.
No kernel may reach another device: no remote copies, remote signals or barrier semaphores. Data moves between devices by JAX's collectives and lax.ppermute only.
A program may use at most 128 MiB of HBM per device.

```python
import math
import jax
import jax.numpy as jnp
import numpy as np
from jax import lax

QUERY_HEADS = 64
KEY_VALUE_HEADS = 8
HEAD_SIZE = 128
TOK_DEV = 256
DOCS = 3
SLOTS = 2
WINDOW_TOKENS = 32768
N_CP = 16
N_GRP = 8


def key_field(key):
    unscaled_scores = jnp.clip(jax.random.normal(jax.random.fold_in(key, 101), (WINDOW_TOKENS, KEY_VALUE_HEADS * HEAD_SIZE), jnp.float32), -4.0, 4.0)
    return unscaled_scores


def draw_keys(key, part):
    return key_field(key).astype(jnp.bfloat16)


def draw_queries(key, part):
    unscaled_scores = jnp.clip(jax.random.normal(jax.random.fold_in(key, 103), (WINDOW_TOKENS, QUERY_HEADS * HEAD_SIZE), jnp.float32), -4.0, 4.0)
    return unscaled_scores.astype(jnp.bfloat16)


def placement(key):
    base = jax.random.fold_in(key, 7)
    device_count = N_CP * N_GRP
    half_peers = N_CP // 2
    group_keys = jax.random.split(jax.random.fold_in(base, 1), N_GRP)
    offsets = jax.vmap(lambda item: jax.random.permutation(item, N_CP)[:half_peers])(group_keys).astype(jnp.int32)
    tile_keys = jax.random.split(jax.random.fold_in(base, 2), device_count)
    tile_order = jax.vmap(lambda item: jax.random.permutation(item, N_CP))(tile_keys).astype(jnp.int32)
    fill_keys = jax.random.split(jax.random.fold_in(base, 3), device_count)
    shuffle = jax.vmap(lambda item: jax.random.permutation(item, N_CP))(fill_keys).astype(jnp.int32)
    device_ids = jnp.arange(device_count, dtype=jnp.int32)
    cp_index = device_ids // N_GRP
    grp_index = device_ids % N_GRP
    device_offsets = offsets[grp_index]
    peer_index = (cp_index[:, None] + device_offsets) % N_CP
    sending = jnp.full((device_count, N_CP, SLOTS), N_CP, jnp.int32)
    sending = sending.at[device_ids[:, None], peer_index].set(tile_order.reshape(device_count, half_peers, SLOTS))
    source_cp = (cp_index[:, None] - device_offsets) % N_CP
    received = source_cp[:, :, None] * SLOTS + jnp.arange(SLOTS, dtype=jnp.int32)[None, None, :]
    taking = jnp.take_along_axis(received.reshape(device_count, N_CP), shuffle, axis=1)
    return (sending.reshape(device_count, N_CP * SLOTS).astype(jnp.int32), taking.astype(jnp.int32))


def draw_send_tile(key, part):
    return placement(key)[0]


def draw_take_slot(key, part):
    return placement(key)[1]


def steps_of(stream_key, shape, cuts, least, high):
    factor_of = 1.0
    for dim, parts in cuts:
        draws = jax.random.uniform(jax.random.fold_in(jax.random.fold_in(stream_key, 6), dim), (parts,), jnp.float32, least / len(cuts), high / len(cuts))
        factor_of = factor_of * jnp.repeat(jnp.exp(draws), shape[dim] // parts).reshape((-1,) + (1,) * (len(shape) - 1 - dim))
    return factor_of


def profile(number_of, total, most, lean):
    portions = [(1 << 20) // math.isqrt(rank ** lean) + 1 for rank in range(2, number_of + 1)]
    rest, given = total - most - (number_of - 1), [1] * (number_of - 1)
    while rest > 0:
        movable = [i for i in range(number_of - 1) if given[i] < most]
        pool, left = sum([portions[i] for i in movable]), rest
        for i in movable:
            more = min(most - given[i], max(1, left * portions[i] // pool), rest)
            given[i] = given[i] + more
            rest = rest - more
    return np.array([most] + given)


def ragged(key, amount, total, bound, skew):
    if amount == 2:
        one = jax.random.randint(key, (), max(1, total - bound), min(bound, total - 1) + 1)
        return jnp.stack([one, total - one])
    sizes = jnp.asarray(profile(amount, total, bound, skew), jnp.int32)
    twos = (amount - 1) // 2
    source_of, sink = sizes[1:1 + 2 * twos:2], sizes[2:2 + 2 * twos:2]
    margin = jnp.minimum(source_of - 1, bound - sink)
    shifted = jax.random.randint(jax.random.fold_in(key, 1), (twos,), 0, 1 << 20) % (margin + 1)
    sizes = sizes.at[1:1 + 2 * twos:2].set(source_of - shifted).at[2:2 + 2 * twos:2].set(sink + shifted)
    return sizes[jax.random.permutation(jax.random.fold_in(key, 2), amount)]


def gaussian(rng, shape, width, reach, cuts=(), kind=jnp.bfloat16):
    values = width * jax.random.normal(rng, shape, jnp.float32)
    if cuts:
        values = values * steps_of(rng, shape, cuts, -0.22, 0.18)
    return jnp.clip(values, -reach, reach).astype(kind)


def setup_inputs(seed: int = 0) -> dict:
    seeds = jax.random.split(jax.random.key(seed), 7)
    return {
        "queries": draw_queries(jax.random.fold_in(seeds[6], 71), 0),
        "keys": draw_keys(jax.random.fold_in(seeds[6], 71), 0),
        "values": gaussian(seeds[2], (WINDOW_TOKENS, KEY_VALUE_HEADS * HEAD_SIZE), 1.0, 6.0, ((0, 128),)),
        "doc_lengths": jax.vmap(lambda own: ragged(own, DOCS, N_GRP * TOK_DEV, N_GRP * TOK_DEV - N_GRP * TOK_DEV // 4, 2))(jax.random.split(seeds[3], N_CP)).reshape((N_CP, DOCS)).astype(jnp.int32),
        "send_tile": draw_send_tile(jax.random.fold_in(seeds[6], 71), 0),
        "take_slot": draw_take_slot(jax.random.fold_in(seeds[6], 71), 0),
    }


def owner_rows(send_tile, take_slot):
    device_count = N_CP * N_GRP
    tile_rows = TOK_DEV // N_CP
    device_ids = jnp.arange(device_count, dtype=jnp.int32)
    cp_index = device_ids // N_GRP
    grp_index = device_ids % N_GRP
    source_cp = take_slot // SLOTS
    source_slot = take_slot % SLOTS
    source_dev = source_cp * N_GRP + grp_index[:, None]
    column = cp_index[:, None] * SLOTS + source_slot
    arrival_tile = send_tile[source_dev, column]
    start = (source_dev * N_CP + arrival_tile) * tile_rows
    offsets = jnp.arange(tile_rows, dtype=jnp.int32)
    return (start[:, :, None] + offsets[None, None, :]).reshape(-1).astype(jnp.int32)

def attend(query_rows, key_rows, value_rows, query_pos, key_pos, query_doc, key_doc):
    queries_per_group = QUERY_HEADS // KEY_VALUE_HEADS
    score_scale = 1.0 / math.sqrt(HEAD_SIZE)
    allowed = (query_doc[:, None] == key_doc[None, :]) & (key_pos[None, :] <= query_pos[:, None])
    pieces = []
    for head_number_index in range(KEY_VALUE_HEADS):
        query_head = query_rows[:, head_number_index * queries_per_group * HEAD_SIZE:(head_number_index + 1) * queries_per_group * HEAD_SIZE]
        query_head = query_head.reshape(-1, queries_per_group, HEAD_SIZE).astype(jnp.float32)
        key_head = key_rows[:, head_number_index * HEAD_SIZE:(head_number_index + 1) * HEAD_SIZE].astype(jnp.float32)
        value_head = value_rows[:, head_number_index * HEAD_SIZE:(head_number_index + 1) * HEAD_SIZE].astype(jnp.float32)
        scores = jnp.einsum('qgd,kd->gqk', query_head, key_head) * score_scale
        scores = jnp.where(allowed[None], scores, -jnp.inf)
        row_max = lax.optimization_barrier(jnp.max(scores, axis=2, keepdims=True))
        weights = jnp.exp(scores - row_max)
        totals = lax.optimization_barrier(jnp.sum(weights, axis=2))
        rounded = lax.optimization_barrier(weights.astype(jnp.bfloat16)).astype(jnp.float32)
        summed = jnp.einsum('gqk,kd->qgd', rounded, value_head)
        mixed = summed / jnp.transpose(totals)[:, :, None]
        pieces.append(mixed.reshape(-1, queries_per_group * HEAD_SIZE))
    return jnp.concatenate(pieces, axis=1).astype(jnp.bfloat16)

def reference(queries, keys, values, doc_lengths, send_tile, take_slot):
    sorted_ordering = owner_rows(send_tile, take_slot)
    group_length = N_GRP * TOK_DEV
    owned_queries = jnp.take(queries, sorted_ordering, axis=0).reshape(N_CP, group_length, QUERY_HEADS * HEAD_SIZE)
    holder_keys = jnp.take(keys, sorted_ordering, axis=0).reshape(N_CP, group_length, KEY_VALUE_HEADS * HEAD_SIZE)
    holder_values = jnp.take(values, sorted_ordering, axis=0).reshape(N_CP, group_length, KEY_VALUE_HEADS * HEAD_SIZE)

    def one_group(inputs):
        group_queries, group_keys, group_values, lengths = inputs
        doc_ends = jnp.cumsum(lengths.astype(jnp.int32)).astype(jnp.int32)
        positions = jnp.arange(group_length, dtype=jnp.int32)
        doc_index = lax.optimization_barrier(jnp.sum((positions[:, None] >= doc_ends[None, :]).astype(jnp.int32), axis=1))
        outputs = []
        for block_index in range(N_GRP):
            first_row = block_index * TOK_DEV
            last_row = first_row + TOK_DEV
            outputs.append(attend(group_queries[first_row:last_row], group_keys[:last_row], group_values[:last_row], positions[first_row:last_row], positions[:last_row], doc_index[first_row:last_row], doc_index[:last_row]))
        return jnp.concatenate(outputs, axis=0)
    attended = lax.map(one_group, (owned_queries, holder_keys, holder_values, doc_lengths))
    return attended.reshape(WINDOW_TOKENS, QUERY_HEADS * HEAD_SIZE)
```

```python
import functools
import math

import jax
import jax.numpy as jnp
from jax import lax
from jax.experimental import pallas as pl
from jax.experimental.pallas import tpu as pltpu
from jax.sharding import PartitionSpec as P

QUERY_HEADS = 64
KEY_VALUE_HEADS = 8
HEAD_SIZE = 128
KEY_BLOCK = 256
MASKED = -1e30


def attention_kernel(bounds, q_ref, k_ref, v_ref, o_ref):
    query_rows = q_ref.shape[0]
    queries_per_group = q_ref.shape[1] // HEAD_SIZE
    score_scale = 1.0 / math.sqrt(HEAD_SIZE)
    first_query = bounds[0]
    lo_block = bounds[1]
    hi_block = bounds[2]
    ends = [bounds[3], bounds[4], bounds[5]]

    def doc_of(pos):
        doc = jnp.zeros(pos.shape, jnp.int32)
        for end in ends:
            doc = doc + (pos >= end).astype(jnp.int32)
        return doc

    query_pos = first_query + lax.broadcasted_iota(jnp.int32, (query_rows, 1), 0)
    query_doc = doc_of(query_pos)

    for head in range(queries_per_group):
        query = q_ref[:, head * HEAD_SIZE:(head + 1) * HEAD_SIZE]

        def body(block, carry):
            row_max, totals, summed = carry
            start = pl.multiple_of(block * KEY_BLOCK, KEY_BLOCK)
            key = k_ref[pl.ds(start, KEY_BLOCK), :]
            value = v_ref[pl.ds(start, KEY_BLOCK), :]
            scores = lax.dot_general(
                query, key, (((1,), (1,)), ((), ())), preferred_element_type=jnp.float32
            ) * score_scale
            key_pos = start + lax.broadcasted_iota(jnp.int32, (1, KEY_BLOCK), 1)
            allowed = (doc_of(key_pos) == query_doc) & (key_pos <= query_pos)
            scores = jnp.where(allowed, scores, MASKED)
            new_max = jnp.maximum(row_max, jnp.max(scores, axis=1, keepdims=True))
            rescale = jnp.exp(row_max - new_max)
            weights = jnp.exp(scores - new_max)
            totals = rescale * totals + jnp.sum(weights, axis=1, keepdims=True)
            summed = rescale * summed + jnp.dot(
                weights.astype(jnp.bfloat16), value, preferred_element_type=jnp.float32
            )
            return new_max, totals, summed

        start_state = (
            jnp.full((query_rows, 1), MASKED, jnp.float32),
            jnp.zeros((query_rows, 1), jnp.float32),
            jnp.zeros((query_rows, HEAD_SIZE), jnp.float32),
        )
        _, totals, summed = lax.fori_loop(lo_block, hi_block, body, start_state)
        o_ref[:, head * HEAD_SIZE:(head + 1) * HEAD_SIZE] = (summed / totals).astype(o_ref.dtype)


def attention(bounds, own_queries, all_keys, all_values, interpret=False):
    tok_rows = own_queries.shape[0]
    group_length = all_keys.shape[0]
    head_width = own_queries.shape[1] // KEY_VALUE_HEADS
    return pl.pallas_call(
        attention_kernel,
        out_shape=jax.ShapeDtypeStruct(own_queries.shape, own_queries.dtype),
        grid_spec=pltpu.PrefetchScalarGridSpec(
            num_scalar_prefetch=1,
            grid=(KEY_VALUE_HEADS,),
            in_specs=[
                pl.BlockSpec((tok_rows, head_width), lambda h, b: (0, h)),
                pl.BlockSpec((group_length, HEAD_SIZE), lambda h, b: (0, h)),
                pl.BlockSpec((group_length, HEAD_SIZE), lambda h, b: (0, h)),
            ],
            out_specs=pl.BlockSpec((tok_rows, head_width), lambda h, b: (0, h)),
        ),
        compiler_params=pltpu.CompilerParams(dimension_semantics=("arbitrary",)),
        interpret=interpret,
    )(bounds, own_queries, all_keys, all_values)


def block_bounds(doc_lengths_row, first_query, tok_rows):
    doc_ends = jnp.cumsum(doc_lengths_row).astype(jnp.int32)
    doc_start = jnp.max(jnp.where(doc_ends <= first_query, doc_ends, 0))
    lo_block = doc_start // KEY_BLOCK
    hi_block = (first_query + tok_rows + KEY_BLOCK - 1) // KEY_BLOCK
    head = jnp.stack([first_query, lo_block, hi_block]).astype(jnp.int32)
    return jnp.concatenate([head, doc_ends, jnp.zeros((2,), jnp.int32)])


def local(queries, keys, values, doc_lengths, send_tile, take_slot):
    tok_rows = queries.shape[0]
    peer_count = lax.axis_size("cp")
    tile_rows = tok_rows // peer_count
    slot_count = send_tile.shape[1] // peer_count
    chosen = send_tile[0]
    placed = take_slot[0]

    def outgoing(source):
        tiled = source.reshape(peer_count, tile_rows, source.shape[1])
        picked = jnp.take(tiled, chosen, axis=0, mode="fill", fill_value=0)
        return picked.reshape(peer_count * slot_count * tile_rows, source.shape[1])

    def incoming(source):
        tiled = source.reshape(peer_count * slot_count, tile_rows, source.shape[1])
        return jnp.take(tiled, placed, axis=0).reshape(tok_rows, source.shape[1])

    got_queries, got_keys, got_values = (
        lax.all_to_all(outgoing(queries), "cp", split_axis=0, concat_axis=0, tiled=True),
        lax.all_to_all(outgoing(keys), "cp", split_axis=0, concat_axis=0, tiled=True),
        lax.all_to_all(outgoing(values), "cp", split_axis=0, concat_axis=0, tiled=True),
    )
    own_queries = incoming(got_queries)
    all_keys, all_values = (
        lax.all_gather(incoming(got_keys), "grp", axis=0, tiled=True),
        lax.all_gather(incoming(got_values), "grp", axis=0, tiled=True),
    )
    member = lax.axis_index("grp")
    bounds = block_bounds(doc_lengths[0], member * tok_rows, tok_rows)
    return attention(bounds, own_queries, all_keys, all_values)


def solution(mesh):
    return jax.shard_map(
        local,
        mesh=mesh,
        in_specs=(
            P(("cp", "grp"), None),
            P(("cp", "grp"), None),
            P(("cp", "grp"), None),
            P("cp", None),
            P(("cp", "grp"), None),
            P(("cp", "grp"), None),
        ),
        out_specs=P(("cp", "grp"), None),
        check_vma=False,
    )
```

```python
import functools
import math

import jax
import jax.numpy as jnp
from jax import lax
from jax.experimental import pallas as pl
from jax.experimental.pallas import tpu as pltpu
from jax.sharding import PartitionSpec as P

QUERY_HEADS = 64
KEY_VALUE_HEADS = 8
HEAD_SIZE = 128
KEY_BLOCK = 256
MASKED = -1e30


def attention_kernel(bounds, q_ref, k_ref, v_ref, o_ref):
    query_rows = q_ref.shape[0]
    queries_per_group = q_ref.shape[1] // HEAD_SIZE
    score_scale = 1.0 / math.sqrt(HEAD_SIZE)
    first_query = bounds[0]
    ends = [bounds[5], bounds[6], bounds[7]]

    query_pos = first_query + lax.broadcasted_iota(jnp.int32, (query_rows, 1), 0)
    query_start = jnp.zeros((query_rows, 1), jnp.int32)
    for end in ends:
        query_start = jnp.maximum(query_start, jnp.where(query_pos >= end, end, 0))

    for head in range(queries_per_group):
        query = q_ref[:, head * HEAD_SIZE:(head + 1) * HEAD_SIZE]

        def body(block, carry, masked):
            row_max, totals, summed = carry
            start = pl.multiple_of(block * KEY_BLOCK, KEY_BLOCK)
            key = k_ref[pl.ds(start, KEY_BLOCK), :]
            value = v_ref[pl.ds(start, KEY_BLOCK), :]
            scores = lax.dot_general(
                query, key, (((1,), (1,)), ((), ())), preferred_element_type=jnp.float32
            ) * score_scale
            if masked:
                key_pos = start + lax.broadcasted_iota(jnp.int32, (1, KEY_BLOCK), 1)
                allowed = (key_pos >= query_start) & (key_pos <= query_pos)
                scores = jnp.where(allowed, scores, MASKED)
            new_max = jnp.maximum(row_max, jnp.max(scores, axis=1, keepdims=True))
            rescale = jnp.exp(row_max - new_max)
            weights = jnp.exp(scores - new_max)
            totals = rescale * totals + jnp.sum(weights, axis=1, keepdims=True)
            summed = rescale * summed + jnp.dot(
                weights.astype(jnp.bfloat16), value, preferred_element_type=jnp.float32
            )
            return new_max, totals, summed

        state = (
            jnp.full((query_rows, 1), MASKED, jnp.float32),
            jnp.zeros((query_rows, 1), jnp.float32),
            jnp.zeros((query_rows, HEAD_SIZE), jnp.float32),
        )
        masked_body = functools.partial(body, masked=True)
        state = lax.fori_loop(bounds[1], bounds[2], masked_body, state)
        state = lax.fori_loop(bounds[2], bounds[3], functools.partial(body, masked=False), state)
        _, totals, summed = lax.fori_loop(bounds[3], bounds[4], masked_body, state)
        o_ref[:, head * HEAD_SIZE:(head + 1) * HEAD_SIZE] = (summed / totals).astype(o_ref.dtype)


def attention(bounds, own_queries, all_keys, all_values, interpret=False):
    tok_rows = own_queries.shape[0]
    group_length = all_keys.shape[0]
    head_width = own_queries.shape[1] // KEY_VALUE_HEADS
    return pl.pallas_call(
        attention_kernel,
        out_shape=jax.ShapeDtypeStruct(own_queries.shape, own_queries.dtype),
        grid_spec=pltpu.PrefetchScalarGridSpec(
            num_scalar_prefetch=1,
            grid=(KEY_VALUE_HEADS,),
            in_specs=[
                pl.BlockSpec((tok_rows, head_width), lambda h, b: (0, h)),
                pl.BlockSpec((group_length, HEAD_SIZE), lambda h, b: (0, h)),
                pl.BlockSpec((group_length, HEAD_SIZE), lambda h, b: (0, h)),
            ],
            out_specs=pl.BlockSpec((tok_rows, head_width), lambda h, b: (0, h)),
        ),
        compiler_params=pltpu.CompilerParams(dimension_semantics=("arbitrary",)),
        interpret=interpret,
    )(bounds, own_queries, all_keys, all_values)


def block_bounds(doc_lengths_row, first_query, tok_rows):
    doc_ends = jnp.cumsum(doc_lengths_row).astype(jnp.int32)

    def doc_start(pos):
        return jnp.max(jnp.where(doc_ends <= pos, doc_ends, 0))

    diagonal = first_query // KEY_BLOCK
    lo_block = doc_start(first_query) // KEY_BLOCK
    full_block = (doc_start(first_query + tok_rows - 1) + KEY_BLOCK - 1) // KEY_BLOCK
    full_block = jnp.clip(full_block, lo_block, diagonal)
    hi_block = (first_query + tok_rows + KEY_BLOCK - 1) // KEY_BLOCK
    head = jnp.stack([first_query, lo_block, full_block, diagonal, hi_block]).astype(jnp.int32)
    return jnp.concatenate([head, doc_ends])


def local(queries, keys, values, doc_lengths, send_tile, take_slot):
    tok_rows = queries.shape[0]
    peer_count = lax.axis_size("cp")
    tile_rows = tok_rows // peer_count
    slot_count = send_tile.shape[1] // peer_count
    chosen = send_tile[0]
    placed = take_slot[0]

    def outgoing(source):
        tiled = source.reshape(peer_count, tile_rows, source.shape[1])
        picked = jnp.take(tiled, chosen, axis=0, mode="fill", fill_value=0)
        return picked.reshape(peer_count * slot_count * tile_rows, source.shape[1])

    def incoming(source):
        tiled = source.reshape(peer_count * slot_count, tile_rows, source.shape[1])
        return jnp.take(tiled, placed, axis=0).reshape(tok_rows, source.shape[1])

    got_queries, got_keys, got_values = (
        lax.all_to_all(outgoing(queries), "cp", split_axis=0, concat_axis=0, tiled=True),
        lax.all_to_all(outgoing(keys), "cp", split_axis=0, concat_axis=0, tiled=True),
        lax.all_to_all(outgoing(values), "cp", split_axis=0, concat_axis=0, tiled=True),
    )
    own_queries = incoming(got_queries)
    all_keys, all_values = (
        lax.all_gather(incoming(got_keys), "grp", axis=0, tiled=True),
        lax.all_gather(incoming(got_values), "grp", axis=0, tiled=True),
    )
    member = lax.axis_index("grp")
    bounds = block_bounds(doc_lengths[0], member * tok_rows, tok_rows)
    return attention(bounds, own_queries, all_keys, all_values)


def solution(mesh):
    return jax.shard_map(
        local,
        mesh=mesh,
        in_specs=(
            P(("cp", "grp"), None),
            P(("cp", "grp"), None),
            P(("cp", "grp"), None),
            P("cp", None),
            P(("cp", "grp"), None),
            P(("cp", "grp"), None),
        ),
        out_specs=P(("cp", "grp"), None),
        check_vma=False,
    )
```

```python
import functools
import math

import jax
import jax.numpy as jnp
from jax import lax
from jax.experimental import pallas as pl
from jax.experimental.pallas import tpu as pltpu
from jax.sharding import PartitionSpec as P

QUERY_HEADS = 64
KEY_VALUE_HEADS = 8
HEAD_SIZE = 128
KEY_BLOCK = 512
LANES = 128
MASKED = -1e30


def attention_kernel(bounds, q_ref, k_ref, v_ref, o_ref, max_ref, total_ref, sum_ref):
    query_rows = q_ref.shape[0]
    queries_per_group = q_ref.shape[1] // HEAD_SIZE
    exp2_scale = math.log2(math.e) / math.sqrt(HEAD_SIZE)
    first_query = bounds[0]
    ends = [bounds[5], bounds[6], bounds[7]]

    query_pos = first_query + lax.broadcasted_iota(jnp.int32, (query_rows, 1), 0)
    query_start = jnp.zeros((query_rows, 1), jnp.int32)
    for end in ends:
        query_start = jnp.maximum(query_start, jnp.where(query_pos >= end, end, 0))

    max_ref[...] = jnp.full(max_ref.shape, MASKED, jnp.float32)
    total_ref[...] = jnp.zeros(total_ref.shape, jnp.float32)
    sum_ref[...] = jnp.zeros(sum_ref.shape, jnp.float32)

    def body(block, carry, masked):
        start = pl.multiple_of(block * KEY_BLOCK, KEY_BLOCK)
        key = k_ref[pl.ds(start, KEY_BLOCK), :]
        value = v_ref[pl.ds(start, KEY_BLOCK), :]
        if masked:
            key_pos = start + lax.broadcasted_iota(jnp.int32, (1, KEY_BLOCK), 1)
            allowed = (key_pos >= query_start) & (key_pos <= query_pos)
        for head in range(queries_per_group):
            query = q_ref[:, head * HEAD_SIZE:(head + 1) * HEAD_SIZE]
            scores = lax.dot_general(
                query, key, (((1,), (1,)), ((), ())), preferred_element_type=jnp.float32
            ) * exp2_scale
            if masked:
                scores = jnp.where(allowed, scores, MASKED)
            row_max = max_ref[head]
            new_max = jnp.maximum(row_max, jnp.max(scores, axis=1, keepdims=True))
            rescale = jnp.exp2(row_max - new_max)
            weights = jnp.exp2(scores - jnp.tile(new_max, (1, KEY_BLOCK // LANES)))
            total_ref[head] = rescale * total_ref[head] + jnp.sum(weights, axis=1, keepdims=True)
            sum_ref[head] = rescale * sum_ref[head] + jnp.dot(
                weights.astype(jnp.bfloat16), value, preferred_element_type=jnp.float32
            )
            max_ref[head] = new_max
        return carry

    masked_body = functools.partial(body, masked=True)
    lax.fori_loop(bounds[1], bounds[2], masked_body, 0)
    lax.fori_loop(bounds[2], bounds[3], functools.partial(body, masked=False), 0)
    lax.fori_loop(bounds[3], bounds[4], masked_body, 0)
    for head in range(queries_per_group):
        o_ref[:, head * HEAD_SIZE:(head + 1) * HEAD_SIZE] = (
            sum_ref[head] / total_ref[head]
        ).astype(o_ref.dtype)


def attention(bounds, own_queries, all_keys, all_values, interpret=False):
    tok_rows = own_queries.shape[0]
    group_length = all_keys.shape[0]
    head_width = own_queries.shape[1] // KEY_VALUE_HEADS
    queries_per_group = head_width // HEAD_SIZE
    return pl.pallas_call(
        attention_kernel,
        out_shape=jax.ShapeDtypeStruct(own_queries.shape, own_queries.dtype),
        grid_spec=pltpu.PrefetchScalarGridSpec(
            num_scalar_prefetch=1,
            grid=(KEY_VALUE_HEADS,),
            in_specs=[
                pl.BlockSpec((tok_rows, head_width), lambda h, b: (0, h)),
                pl.BlockSpec((group_length, HEAD_SIZE), lambda h, b: (0, h)),
                pl.BlockSpec((group_length, HEAD_SIZE), lambda h, b: (0, h)),
            ],
            out_specs=pl.BlockSpec((tok_rows, head_width), lambda h, b: (0, h)),
            scratch_shapes=[
                pltpu.VMEM((queries_per_group, tok_rows, LANES), jnp.float32),
                pltpu.VMEM((queries_per_group, tok_rows, LANES), jnp.float32),
                pltpu.VMEM((queries_per_group, tok_rows, HEAD_SIZE), jnp.float32),
            ],
        ),
        compiler_params=pltpu.CompilerParams(dimension_semantics=("arbitrary",)),
        interpret=interpret,
    )(bounds, own_queries, all_keys, all_values)


def block_bounds(doc_lengths_row, first_query, tok_rows):
    doc_ends = jnp.cumsum(doc_lengths_row).astype(jnp.int32)

    def doc_start(pos):
        return jnp.max(jnp.where(doc_ends <= pos, doc_ends, 0))

    diagonal = first_query // KEY_BLOCK
    lo_block = doc_start(first_query) // KEY_BLOCK
    full_block = (doc_start(first_query + tok_rows - 1) + KEY_BLOCK - 1) // KEY_BLOCK
    full_block = jnp.clip(full_block, lo_block, diagonal)
    hi_block = (first_query + tok_rows + KEY_BLOCK - 1) // KEY_BLOCK
    head = jnp.stack([first_query, lo_block, full_block, diagonal, hi_block]).astype(jnp.int32)
    return jnp.concatenate([head, doc_ends])


def local(queries, keys, values, doc_lengths, send_tile, take_slot):
    tok_rows = queries.shape[0]
    peer_count = lax.axis_size("cp")
    tile_rows = tok_rows // peer_count
    slot_count = send_tile.shape[1] // peer_count
    chosen = send_tile[0]
    placed = take_slot[0]

    def outgoing(source):
        tiled = source.reshape(peer_count, tile_rows, source.shape[1])
        picked = jnp.take(tiled, chosen, axis=0, mode="fill", fill_value=0)
        return picked.reshape(peer_count * slot_count * tile_rows, source.shape[1])

    def incoming(source):
        tiled = source.reshape(peer_count * slot_count, tile_rows, source.shape[1])
        return jnp.take(tiled, placed, axis=0).reshape(tok_rows, source.shape[1])

    got_queries, got_keys, got_values = (
        lax.all_to_all(outgoing(queries), "cp", split_axis=0, concat_axis=0, tiled=True),
        lax.all_to_all(outgoing(keys), "cp", split_axis=0, concat_axis=0, tiled=True),
        lax.all_to_all(outgoing(values), "cp", split_axis=0, concat_axis=0, tiled=True),
    )
    own_queries = incoming(got_queries)
    all_keys, all_values = (
        lax.all_gather(incoming(got_keys), "grp", axis=0, tiled=True),
        lax.all_gather(incoming(got_values), "grp", axis=0, tiled=True),
    )
    member = lax.axis_index("grp")
    bounds = block_bounds(doc_lengths[0], member * tok_rows, tok_rows)
    return attention(bounds, own_queries, all_keys, all_values)


def solution(mesh):
    return jax.shard_map(
        local,
        mesh=mesh,
        in_specs=(
            P(("cp", "grp"), None),
            P(("cp", "grp"), None),
            P(("cp", "grp"), None),
            P("cp", None),
            P(("cp", "grp"), None),
            P(("cp", "grp"), None),
        ),
        out_specs=P(("cp", "grp"), None),
        check_vma=False,
    )
```

```python
import functools
import math

import jax
import jax.numpy as jnp
from jax import lax
from jax.experimental import pallas as pl
from jax.experimental.pallas import tpu as pltpu
from jax.sharding import PartitionSpec as P

QUERY_HEADS = 64
KEY_VALUE_HEADS = 8
HEAD_SIZE = 128
KEY_BLOCK = 512
LANES = 128
MASKED = -1e30


def attention_kernel(bounds, q_ref, k_ref, v_ref, *refs, previous=False):
    if previous:
        refs = refs[1:]
    o_ref, max_ref, total_ref, sum_ref = refs
    query_rows = q_ref.shape[0]
    queries_per_group = q_ref.shape[1] // HEAD_SIZE
    exp2_scale = math.log2(math.e) / math.sqrt(HEAD_SIZE)
    first_query = bounds[0]
    ends = [bounds[5], bounds[6], bounds[7]]

    query_pos = first_query + lax.broadcasted_iota(jnp.int32, (query_rows, 1), 0)
    query_start = jnp.zeros((query_rows, 1), jnp.int32)
    for end in ends:
        query_start = jnp.maximum(query_start, jnp.where(query_pos >= end, end, 0))

    max_ref[...] = jnp.full(max_ref.shape, MASKED, jnp.float32)
    total_ref[...] = jnp.zeros(total_ref.shape, jnp.float32)
    sum_ref[...] = jnp.zeros(sum_ref.shape, jnp.float32)

    def body(block, carry, masked):
        start = pl.multiple_of(block * KEY_BLOCK, KEY_BLOCK)
        key = k_ref[pl.ds(start, KEY_BLOCK), :]
        value = v_ref[pl.ds(start, KEY_BLOCK), :]
        if masked:
            key_pos = start + lax.broadcasted_iota(jnp.int32, (1, KEY_BLOCK), 1)
            allowed = (key_pos >= query_start) & (key_pos <= query_pos)
        for head in range(queries_per_group):
            query = q_ref[:, head * HEAD_SIZE:(head + 1) * HEAD_SIZE]
            scores = lax.dot_general(
                query, key, (((1,), (1,)), ((), ())), preferred_element_type=jnp.float32
            ) * exp2_scale
            if masked:
                scores = jnp.where(allowed, scores, MASKED)
            row_max = max_ref[head]
            new_max = jnp.maximum(row_max, jnp.max(scores, axis=1, keepdims=True))
            rescale = jnp.exp2(row_max - new_max)
            weights = jnp.exp2(scores - jnp.tile(new_max, (1, KEY_BLOCK // LANES)))
            total_ref[head] = rescale * total_ref[head] + jnp.sum(weights, axis=1, keepdims=True)
            sum_ref[head] = rescale * sum_ref[head] + jnp.dot(
                weights.astype(jnp.bfloat16), value, preferred_element_type=jnp.float32
            )
            max_ref[head] = new_max
        return carry

    masked_body = functools.partial(body, masked=True)
    lax.fori_loop(bounds[1], bounds[2], masked_body, 0)
    lax.fori_loop(bounds[2], bounds[3], functools.partial(body, masked=False), 0)
    lax.fori_loop(bounds[3], bounds[4], masked_body, 0)
    for head in range(queries_per_group):
        o_ref[:, head * HEAD_SIZE:(head + 1) * HEAD_SIZE] = (
            sum_ref[head] / total_ref[head]
        ).astype(o_ref.dtype)


def attention(bounds, own_queries, all_kv, head_offset, previous=None, interpret=False):
    tok_rows = own_queries.shape[0]
    group_length = all_kv.shape[0]
    kv_heads = all_kv.shape[1] // (2 * HEAD_SIZE)
    head_width = QUERY_HEADS // KEY_VALUE_HEADS * HEAD_SIZE
    call_heads = own_queries.shape[1] // head_width
    queries_per_group = head_width // HEAD_SIZE
    in_specs = [
        pl.BlockSpec((tok_rows, head_width), lambda h, b: (0, h)),
        pl.BlockSpec((group_length, HEAD_SIZE), lambda h, b: (0, h + head_offset)),
        pl.BlockSpec((group_length, HEAD_SIZE), lambda h, b: (0, h + head_offset + kv_heads)),
    ]
    operands = [bounds, own_queries, all_kv, all_kv]
    aliases = {}
    if previous is not None:
        in_specs.append(pl.BlockSpec(memory_space=pl.ANY))
        operands.append(previous)
        aliases = {4: 0}
    return pl.pallas_call(
        attention_kernel if previous is None else functools.partial(attention_kernel, previous=True),
        out_shape=jax.ShapeDtypeStruct((tok_rows, kv_heads * head_width), own_queries.dtype),
        grid_spec=pltpu.PrefetchScalarGridSpec(
            num_scalar_prefetch=1,
            grid=(call_heads,),
            in_specs=in_specs,
            out_specs=pl.BlockSpec((tok_rows, head_width), lambda h, b: (0, h + head_offset)),
            scratch_shapes=[
                pltpu.VMEM((queries_per_group, tok_rows, LANES), jnp.float32),
                pltpu.VMEM((queries_per_group, tok_rows, LANES), jnp.float32),
                pltpu.VMEM((queries_per_group, tok_rows, HEAD_SIZE), jnp.float32),
            ],
        ),
        input_output_aliases=aliases,
        cost_estimate=pl.CostEstimate(
            flops=4 * call_heads * queries_per_group * tok_rows * group_length * HEAD_SIZE,
            transcendentals=call_heads * queries_per_group * tok_rows * group_length,
            bytes_accessed=2 * own_queries.size * 2 + 2 * call_heads * group_length * HEAD_SIZE * 2,
        ),
        compiler_params=pltpu.CompilerParams(dimension_semantics=("arbitrary",)),
        interpret=interpret,
    )(*operands)


def block_bounds(doc_lengths_row, first_query, tok_rows):
    doc_ends = jnp.cumsum(doc_lengths_row).astype(jnp.int32)

    def doc_start(pos):
        return jnp.max(jnp.where(doc_ends <= pos, doc_ends, 0))

    diagonal = first_query // KEY_BLOCK
    lo_block = doc_start(first_query) // KEY_BLOCK
    full_block = (doc_start(first_query + tok_rows - 1) + KEY_BLOCK - 1) // KEY_BLOCK
    full_block = jnp.clip(full_block, lo_block, diagonal)
    hi_block = (first_query + tok_rows + KEY_BLOCK - 1) // KEY_BLOCK
    head = jnp.stack([first_query, lo_block, full_block, diagonal, hi_block]).astype(jnp.int32)
    return jnp.concatenate([head, doc_ends])


def local(queries, keys, values, doc_lengths, send_tile, take_slot):
    tok_rows = queries.shape[0]
    peer_count = lax.axis_size("cp")
    tile_rows = tok_rows // peer_count
    slot_count = send_tile.shape[1] // peer_count
    chosen = send_tile[0]
    placed = take_slot[0]

    def outgoing(source):
        tiled = source.reshape(peer_count, tile_rows, source.shape[1])
        picked = jnp.take(tiled, chosen, axis=0, mode="clip")
        return picked.reshape(peer_count * slot_count * tile_rows, source.shape[1])

    def incoming(source):
        tiled = source.reshape(peer_count * slot_count, tile_rows, source.shape[1])
        return jnp.take(tiled, placed, axis=0, mode="clip").reshape(tok_rows, source.shape[1])

    def relayout(source):
        sent = outgoing(source)
        return incoming(lax.all_to_all(sent, "cp", split_axis=0, concat_axis=0, tiled=True))

    own_kv = relayout(jnp.concatenate([keys, values], axis=1))
    all_kv = lax.all_gather(own_kv, "grp", axis=0, tiled=True)
    half = queries.shape[1] // 2
    first_queries = relayout(queries[:, :half])
    second_queries = relayout(queries[:, half:])
    member = lax.axis_index("grp")
    bounds = block_bounds(doc_lengths[0], member * tok_rows, tok_rows)
    half_heads = KEY_VALUE_HEADS // 2
    attended = attention(bounds, first_queries, all_kv, 0)
    return attention(bounds, second_queries, all_kv, half_heads, previous=attended)


def solution(mesh):
    return jax.shard_map(
        local,
        mesh=mesh,
        in_specs=(
            P(("cp", "grp"), None),
            P(("cp", "grp"), None),
            P(("cp", "grp"), None),
            P("cp", None),
            P(("cp", "grp"), None),
            P(("cp", "grp"), None),
        ),
        out_specs=P(("cp", "grp"), None),
        check_vma=False,
    )
```

```python
import functools
import math

import jax
import jax.numpy as jnp
from jax import lax
from jax.experimental import pallas as pl
from jax.experimental.pallas import tpu as pltpu
from jax.sharding import PartitionSpec as P


QUERY_HEADS = 64
KEY_VALUE_HEADS = 8
HEAD_SIZE = 128
KEY_BLOCK = 512
LANES = 128
MASKED = -1e30


def attention_kernel(bounds, q_ref, k_ref, v_ref, *refs, previous=False):
    if previous:
        refs = refs[1:]
    o_ref, max_ref, total_ref, sum_ref = refs
    query_rows = q_ref.shape[0]
    queries_per_group = q_ref.shape[1] // HEAD_SIZE
    exp2_scale = math.log2(math.e) / math.sqrt(HEAD_SIZE)
    first_query = bounds[0]
    ends = [bounds[5], bounds[6], bounds[7]]

    query_pos = first_query + lax.broadcasted_iota(jnp.int32, (query_rows, 1), 0)
    query_start = jnp.zeros((query_rows, 1), jnp.int32)
    for end in ends:
        query_start = jnp.maximum(query_start, jnp.where(query_pos >= end, end, 0))

    max_ref[...] = jnp.full(max_ref.shape, MASKED, jnp.float32)
    total_ref[...] = jnp.zeros(total_ref.shape, jnp.float32)
    sum_ref[...] = jnp.zeros(sum_ref.shape, jnp.float32)

    def body(block, carry, masked):
        start = pl.multiple_of(block * KEY_BLOCK, KEY_BLOCK)
        key = k_ref[pl.ds(start, KEY_BLOCK), :]
        value = v_ref[pl.ds(start, KEY_BLOCK), :]
        if masked:
            key_pos = start + lax.broadcasted_iota(jnp.int32, (1, KEY_BLOCK), 1)
            allowed = (key_pos >= query_start) & (key_pos <= query_pos)
        for head in range(queries_per_group):
            query = q_ref[:, head * HEAD_SIZE:(head + 1) * HEAD_SIZE]
            scores = lax.dot_general(
                query, key, (((1,), (1,)), ((), ())), preferred_element_type=jnp.float32
            ) * exp2_scale
            if masked:
                scores = jnp.where(allowed, scores, MASKED)
            row_max = max_ref[head]
            new_max = jnp.maximum(row_max, jnp.max(scores, axis=1, keepdims=True))
            rescale = jnp.exp2(row_max - new_max)
            weights = jnp.exp2(scores - jnp.tile(new_max, (1, KEY_BLOCK // LANES)))
            total_ref[head] = rescale * total_ref[head] + jnp.sum(weights, axis=1, keepdims=True)
            sum_ref[head] = rescale * sum_ref[head] + jnp.dot(
                weights.astype(jnp.bfloat16), value, preferred_element_type=jnp.float32
            )
            max_ref[head] = new_max
        return carry

    masked_body = functools.partial(body, masked=True)
    lax.fori_loop(bounds[1], bounds[2], masked_body, 0)
    lax.fori_loop(bounds[2], bounds[3], functools.partial(body, masked=False), 0)
    lax.fori_loop(bounds[3], bounds[4], masked_body, 0)
    for head in range(queries_per_group):
        o_ref[:, head * HEAD_SIZE:(head + 1) * HEAD_SIZE] = (
            sum_ref[head] / total_ref[head]
        ).astype(o_ref.dtype)


def attention(bounds, own_queries, all_kv, head_offset, previous=None, interpret=False):
    tok_rows = own_queries.shape[0]
    group_length = all_kv.shape[0]
    kv_heads = all_kv.shape[1] // (2 * HEAD_SIZE)
    head_width = QUERY_HEADS // KEY_VALUE_HEADS * HEAD_SIZE
    call_heads = own_queries.shape[1] // head_width
    queries_per_group = head_width // HEAD_SIZE
    in_specs = [
        pl.BlockSpec((tok_rows, head_width), lambda h, b: (0, h)),
        pl.BlockSpec((group_length, HEAD_SIZE), lambda h, b: (0, h + head_offset)),
        pl.BlockSpec((group_length, HEAD_SIZE), lambda h, b: (0, h + head_offset + kv_heads)),
    ]
    operands = [bounds, own_queries, all_kv, all_kv]
    aliases = {}
    if previous is not None:
        in_specs.append(pl.BlockSpec(memory_space=pl.ANY))
        operands.append(previous)
        aliases = {4: 0}
    return pl.pallas_call(
        attention_kernel if previous is None else functools.partial(attention_kernel, previous=True),
        out_shape=jax.ShapeDtypeStruct((tok_rows, kv_heads * head_width), own_queries.dtype),
        grid_spec=pltpu.PrefetchScalarGridSpec(
            num_scalar_prefetch=1,
            grid=(call_heads,),
            in_specs=in_specs,
            out_specs=pl.BlockSpec((tok_rows, head_width), lambda h, b: (0, h + head_offset)),
            scratch_shapes=[
                pltpu.VMEM((queries_per_group, tok_rows, LANES), jnp.float32),
                pltpu.VMEM((queries_per_group, tok_rows, LANES), jnp.float32),
                pltpu.VMEM((queries_per_group, tok_rows, HEAD_SIZE), jnp.float32),
            ],
        ),
        input_output_aliases=aliases,
        cost_estimate=pl.CostEstimate(
            flops=4 * call_heads * queries_per_group * tok_rows * group_length * HEAD_SIZE,
            transcendentals=call_heads * queries_per_group * tok_rows * group_length,
            bytes_accessed=2 * own_queries.size * 2 + 2 * call_heads * group_length * HEAD_SIZE * 2,
        ),
        compiler_params=pltpu.CompilerParams(dimension_semantics=("arbitrary",)),
        interpret=interpret,
    )(*operands)


def block_bounds(doc_lengths_row, first_query, tok_rows):
    doc_ends = jnp.cumsum(doc_lengths_row).astype(jnp.int32)

    def doc_start(pos):
        return jnp.max(jnp.where(doc_ends <= pos, doc_ends, 0))

    diagonal = first_query // KEY_BLOCK
    lo_block = doc_start(first_query) // KEY_BLOCK
    full_block = (doc_start(first_query + tok_rows - 1) + KEY_BLOCK - 1) // KEY_BLOCK
    full_block = jnp.clip(full_block, lo_block, diagonal)
    hi_block = (first_query + tok_rows + KEY_BLOCK - 1) // KEY_BLOCK
    head = jnp.stack([first_query, lo_block, full_block, diagonal, hi_block]).astype(jnp.int32)
    return jnp.concatenate([head, doc_ends])


def local(queries, keys, values, doc_lengths, send_tile, take_slot):
    tok_rows = queries.shape[0]
    peer_count = lax.axis_size("cp")
    tile_rows = tok_rows // peer_count
    slot_count = send_tile.shape[1] // peer_count
    chosen = send_tile[0]
    placed = take_slot[0]

    def outgoing(source):
        tiled = source.reshape(peer_count, tile_rows, source.shape[1])
        picked = jnp.take(tiled, chosen, axis=0, mode="clip")
        return picked.reshape(peer_count * slot_count * tile_rows, source.shape[1])

    def incoming(source):
        tiled = source.reshape(peer_count * slot_count, tile_rows, source.shape[1])
        return jnp.take(tiled, placed, axis=0, mode="clip").reshape(tok_rows, source.shape[1])

    def relayout(source):
        sent = outgoing(source)
        return incoming(lax.all_to_all(sent, "cp", split_axis=0, concat_axis=0, tiled=True))

    position = lax.axis_index("cp")
    shifted_slot = ((position - placed // slot_count) % peer_count) * slot_count + placed % slot_count

    def relayout_by_shifts(source):
        sent = outgoing(source).reshape(peer_count, slot_count * tile_rows, source.shape[1])
        pieces = [lax.dynamic_index_in_dim(sent, position, 0, keepdims=False)]
        for shift in range(1, peer_count):
            piece = lax.dynamic_index_in_dim(sent, (position + shift) % peer_count, 0, keepdims=False)
            pairs = [(i, (i + shift) % peer_count) for i in range(peer_count)]
            pieces.append(lax.ppermute(piece, "cp", pairs))
        got = jnp.stack(pieces).reshape(peer_count * slot_count, tile_rows, source.shape[1])
        return jnp.take(got, shifted_slot, axis=0, mode="clip").reshape(tok_rows, source.shape[1])

    own_kv = relayout(jnp.concatenate([keys, values], axis=1))
    all_kv = lax.all_gather(own_kv, "grp", axis=0, tiled=True)
    half = queries.shape[1] // 2
    first_queries = relayout_by_shifts(queries[:, :half])
    second_queries = relayout_by_shifts(queries[:, half:])
    member = lax.axis_index("grp")
    bounds = block_bounds(doc_lengths[0], member * tok_rows, tok_rows)
    half_heads = KEY_VALUE_HEADS // 2
    attended = attention(bounds, first_queries, all_kv, 0)
    return attention(bounds, second_queries, all_kv, half_heads, previous=attended)


def solution(mesh):
    return jax.shard_map(
        local,
        mesh=mesh,
        in_specs=(
            P(("cp", "grp"), None),
            P(("cp", "grp"), None),
            P(("cp", "grp"), None),
            P("cp", None),
            P(("cp", "grp"), None),
            P(("cp", "grp"), None),
        ),
        out_specs=P(("cp", "grp"), None),
        check_vma=False,
    )
```

```python
import functools
import math

import jax
import jax.numpy as jnp
from jax import lax
from jax.experimental import pallas as pl
from jax.experimental.pallas import tpu as pltpu
from jax.sharding import PartitionSpec as P

QUERY_HEADS = 64
KEY_VALUE_HEADS = 8
HEAD_SIZE = 128
KEY_BLOCK = 512
LANES = 128
MASKED = -1e30


def attention_kernel(bounds, q_ref, k_ref, v_ref, *refs, previous=False):
    if previous:
        refs = refs[1:]
    o_ref, max_ref, total_ref, sum_ref = refs
    query_rows = q_ref.shape[0]
    queries_per_group = q_ref.shape[1] // HEAD_SIZE
    exp2_scale = math.log2(math.e) / math.sqrt(HEAD_SIZE)
    first_query = bounds[0]
    ends = [bounds[5], bounds[6], bounds[7]]

    query_pos = first_query + lax.broadcasted_iota(jnp.int32, (query_rows, 1), 0)
    query_start = jnp.zeros((query_rows, 1), jnp.int32)
    for end in ends:
        query_start = jnp.maximum(query_start, jnp.where(query_pos >= end, end, 0))

    max_ref[...] = jnp.full(max_ref.shape, MASKED, jnp.float32)
    total_ref[...] = jnp.zeros(total_ref.shape, jnp.float32)
    sum_ref[...] = jnp.zeros(sum_ref.shape, jnp.float32)

    def body(block, carry, masked):
        start = pl.multiple_of(block * KEY_BLOCK, KEY_BLOCK)
        key = k_ref[pl.ds(start, KEY_BLOCK), :]
        value = v_ref[pl.ds(start, KEY_BLOCK), :]
        if masked:
            key_pos = start + lax.broadcasted_iota(jnp.int32, (1, KEY_BLOCK), 1)
            allowed = (key_pos >= query_start) & (key_pos <= query_pos)
        for head in range(queries_per_group):
            query = q_ref[:, head * HEAD_SIZE:(head + 1) * HEAD_SIZE]
            scores = lax.dot_general(
                query, key, (((1,), (1,)), ((), ())), preferred_element_type=jnp.float32
            ) * exp2_scale
            if masked:
                scores = jnp.where(allowed, scores, MASKED)
            row_max = max_ref[head]
            new_max = jnp.maximum(row_max, jnp.max(scores, axis=1, keepdims=True))
            rescale = jnp.exp2(row_max - new_max)
            weights = jnp.exp2(scores - jnp.tile(new_max, (1, KEY_BLOCK // LANES)))
            total_ref[head] = rescale * total_ref[head] + jnp.sum(weights, axis=1, keepdims=True)
            sum_ref[head] = rescale * sum_ref[head] + jnp.dot(
                weights.astype(jnp.bfloat16), value, preferred_element_type=jnp.float32
            )
            max_ref[head] = new_max
        return carry

    masked_body = functools.partial(body, masked=True)
    lax.fori_loop(bounds[1], bounds[2], masked_body, 0)
    lax.fori_loop(bounds[2], bounds[3], functools.partial(body, masked=False), 0)
    lax.fori_loop(bounds[3], bounds[4], masked_body, 0)
    for head in range(queries_per_group):
        o_ref[:, head * HEAD_SIZE:(head + 1) * HEAD_SIZE] = (
            sum_ref[head] / total_ref[head]
        ).astype(o_ref.dtype)


def attention(bounds, own_queries, all_kv, head_offset, previous=None, interpret=False):
    tok_rows = own_queries.shape[0]
    group_length = all_kv.shape[0]
    kv_heads = all_kv.shape[1] // (2 * HEAD_SIZE)
    head_width = QUERY_HEADS // KEY_VALUE_HEADS * HEAD_SIZE
    call_heads = own_queries.shape[1] // head_width
    queries_per_group = head_width // HEAD_SIZE
    in_specs = [
        pl.BlockSpec((tok_rows, head_width), lambda h, b: (0, h)),
        pl.BlockSpec((group_length, HEAD_SIZE), lambda h, b: (0, h + head_offset)),
        pl.BlockSpec((group_length, HEAD_SIZE), lambda h, b: (0, h + head_offset + kv_heads)),
    ]
    operands = [bounds, own_queries, all_kv, all_kv]
    aliases = {}
    if previous is not None:
        in_specs.append(pl.BlockSpec(memory_space=pl.ANY))
        operands.append(previous)
        aliases = {4: 0}
    return pl.pallas_call(
        attention_kernel if previous is None else functools.partial(attention_kernel, previous=True),
        out_shape=jax.ShapeDtypeStruct((tok_rows, kv_heads * head_width), own_queries.dtype),
        grid_spec=pltpu.PrefetchScalarGridSpec(
            num_scalar_prefetch=1,
            grid=(call_heads,),
            in_specs=in_specs,
            out_specs=pl.BlockSpec((tok_rows, head_width), lambda h, b: (0, h + head_offset)),
            scratch_shapes=[
                pltpu.VMEM((queries_per_group, tok_rows, LANES), jnp.float32),
                pltpu.VMEM((queries_per_group, tok_rows, LANES), jnp.float32),
                pltpu.VMEM((queries_per_group, tok_rows, HEAD_SIZE), jnp.float32),
            ],
        ),
        input_output_aliases=aliases,
        cost_estimate=pl.CostEstimate(
            flops=4 * call_heads * queries_per_group * tok_rows * group_length * HEAD_SIZE,
            transcendentals=call_heads * queries_per_group * tok_rows * group_length,
            bytes_accessed=2 * own_queries.size * 2 + 2 * call_heads * group_length * HEAD_SIZE * 2,
        ),
        compiler_params=pltpu.CompilerParams(dimension_semantics=("arbitrary",)),
        interpret=interpret,
    )(*operands)


def block_bounds(doc_lengths_row, first_query, tok_rows):
    doc_ends = jnp.cumsum(doc_lengths_row).astype(jnp.int32)

    def doc_start(pos):
        return jnp.max(jnp.where(doc_ends <= pos, doc_ends, 0))

    diagonal = first_query // KEY_BLOCK
    lo_block = doc_start(first_query) // KEY_BLOCK
    full_block = (doc_start(first_query + tok_rows - 1) + KEY_BLOCK - 1) // KEY_BLOCK
    full_block = jnp.clip(full_block, lo_block, diagonal)
    hi_block = (first_query + tok_rows + KEY_BLOCK - 1) // KEY_BLOCK
    head = jnp.stack([first_query, lo_block, full_block, diagonal, hi_block]).astype(jnp.int32)
    return jnp.concatenate([head, doc_ends])


def local(queries, keys, values, doc_lengths, send_tile, take_slot):
    tok_rows = queries.shape[0]
    peer_count = lax.axis_size("cp")
    tile_rows = tok_rows // peer_count
    slot_count = send_tile.shape[1] // peer_count
    chosen = send_tile[0]
    placed = take_slot[0]

    def outgoing(source):
        tiled = source.reshape(peer_count, tile_rows, source.shape[1])
        picked = jnp.take(tiled, chosen, axis=0, mode="clip")
        return picked.reshape(peer_count * slot_count * tile_rows, source.shape[1])

    def incoming(source):
        tiled = source.reshape(peer_count * slot_count, tile_rows, source.shape[1])
        return jnp.take(tiled, placed, axis=0, mode="clip").reshape(tok_rows, source.shape[1])

    def relayout(source):
        sent = outgoing(source)
        return incoming(lax.all_to_all(sent, "cp", split_axis=0, concat_axis=0, tiled=True))

    half = queries.shape[1] // 2
    first = relayout(jnp.concatenate([queries[:, :half], keys, values], axis=1))
    first_queries = first[:, :half]
    all_kv = lax.all_gather(first[:, half:], "grp", axis=0, tiled=True)
    second_queries = relayout(queries[:, half:])
    member = lax.axis_index("grp")
    bounds = block_bounds(doc_lengths[0], member * tok_rows, tok_rows)
    half_heads = KEY_VALUE_HEADS // 2
    attended = attention(bounds, first_queries, all_kv, 0)
    return attention(bounds, second_queries, all_kv, half_heads, previous=attended)


def solution(mesh):
    return jax.shard_map(
        local,
        mesh=mesh,
        in_specs=(
            P(("cp", "grp"), None),
            P(("cp", "grp"), None),
            P(("cp", "grp"), None),
            P("cp", None),
            P(("cp", "grp"), None),
            P(("cp", "grp"), None),
        ),
        out_specs=P(("cp", "grp"), None),
        check_vma=False,
    )
```

```python
import functools
import math

import jax
import jax.numpy as jnp
from jax import lax
from jax.experimental import pallas as pl
from jax.experimental.pallas import tpu as pltpu
from jax.sharding import PartitionSpec as P

QUERY_HEADS = 64
KEY_VALUE_HEADS = 8
HEAD_SIZE = 128
KEY_BLOCK = 1024
LANES = 128
MASKED = -1e30


def attention_kernel(bounds, q_ref, k_ref, v_ref, *refs, previous=False):
    if previous:
        refs = refs[1:]
    o_ref, max_ref, total_ref, sum_ref = refs
    query_rows = q_ref.shape[0]
    queries_per_group = q_ref.shape[1] // HEAD_SIZE
    exp2_scale = math.log2(math.e) / math.sqrt(HEAD_SIZE)
    first_query = bounds[0]
    ends = [bounds[5], bounds[6], bounds[7]]

    query_pos = first_query + lax.broadcasted_iota(jnp.int32, (query_rows, 1), 0)
    query_start = jnp.zeros((query_rows, 1), jnp.int32)
    for end in ends:
        query_start = jnp.maximum(query_start, jnp.where(query_pos >= end, end, 0))

    max_ref[...] = jnp.full(max_ref.shape, MASKED, jnp.float32)
    total_ref[...] = jnp.zeros(total_ref.shape, jnp.float32)
    sum_ref[...] = jnp.zeros(sum_ref.shape, jnp.float32)

    def body(block, carry, masked):
        start = pl.multiple_of(block * KEY_BLOCK, KEY_BLOCK)
        key = k_ref[pl.ds(start, KEY_BLOCK), :]
        value = v_ref[pl.ds(start, KEY_BLOCK), :]
        if masked:
            key_pos = start + lax.broadcasted_iota(jnp.int32, (1, KEY_BLOCK), 1)
            allowed = (key_pos >= query_start) & (key_pos <= query_pos)
        for head in range(queries_per_group):
            query = q_ref[:, head * HEAD_SIZE:(head + 1) * HEAD_SIZE]
            scores = lax.dot_general(
                query, key, (((1,), (1,)), ((), ())), preferred_element_type=jnp.float32
            ) * exp2_scale
            if masked:
                scores = jnp.where(allowed, scores, MASKED)
            row_max = max_ref[head]
            new_max = jnp.maximum(row_max, jnp.max(scores, axis=1, keepdims=True))
            rescale = jnp.exp2(row_max - new_max)
            weights = jnp.exp2(scores - jnp.tile(new_max, (1, KEY_BLOCK // LANES)))
            total_ref[head] = rescale * total_ref[head] + jnp.sum(weights, axis=1, keepdims=True)
            sum_ref[head] = rescale * sum_ref[head] + jnp.dot(
                weights.astype(jnp.bfloat16), value, preferred_element_type=jnp.float32
            )
            max_ref[head] = new_max
        return carry

    masked_body = functools.partial(body, masked=True)
    lax.fori_loop(bounds[1], bounds[2], masked_body, 0)
    lax.fori_loop(bounds[2], bounds[3], functools.partial(body, masked=False), 0)
    lax.fori_loop(bounds[3], bounds[4], masked_body, 0)
    for head in range(queries_per_group):
        o_ref[:, head * HEAD_SIZE:(head + 1) * HEAD_SIZE] = (
            sum_ref[head] / total_ref[head]
        ).astype(o_ref.dtype)


def attention(bounds, own_queries, all_kv, head_offset, previous=None, interpret=False):
    tok_rows = own_queries.shape[0]
    group_length = all_kv.shape[0]
    kv_heads = all_kv.shape[1] // (2 * HEAD_SIZE)
    head_width = QUERY_HEADS // KEY_VALUE_HEADS * HEAD_SIZE
    call_heads = own_queries.shape[1] // head_width
    queries_per_group = head_width // HEAD_SIZE
    in_specs = [
        pl.BlockSpec((tok_rows, head_width), lambda h, b: (0, h)),
        pl.BlockSpec((group_length, HEAD_SIZE), lambda h, b: (0, h + head_offset)),
        pl.BlockSpec((group_length, HEAD_SIZE), lambda h, b: (0, h + head_offset + kv_heads)),
    ]
    operands = [bounds, own_queries, all_kv, all_kv]
    aliases = {}
    if previous is not None:
        in_specs.append(pl.BlockSpec(memory_space=pl.ANY))
        operands.append(previous)
        aliases = {4: 0}
    return pl.pallas_call(
        attention_kernel if previous is None else functools.partial(attention_kernel, previous=True),
        out_shape=jax.ShapeDtypeStruct((tok_rows, kv_heads * head_width), own_queries.dtype),
        grid_spec=pltpu.PrefetchScalarGridSpec(
            num_scalar_prefetch=1,
            grid=(call_heads,),
            in_specs=in_specs,
            out_specs=pl.BlockSpec((tok_rows, head_width), lambda h, b: (0, h + head_offset)),
            scratch_shapes=[
                pltpu.VMEM((queries_per_group, tok_rows, LANES), jnp.float32),
                pltpu.VMEM((queries_per_group, tok_rows, LANES), jnp.float32),
                pltpu.VMEM((queries_per_group, tok_rows, HEAD_SIZE), jnp.float32),
            ],
        ),
        input_output_aliases=aliases,
        cost_estimate=pl.CostEstimate(
            flops=4 * call_heads * queries_per_group * tok_rows * group_length * HEAD_SIZE,
            transcendentals=call_heads * queries_per_group * tok_rows * group_length,
            bytes_accessed=2 * own_queries.size * 2 + 2 * call_heads * group_length * HEAD_SIZE * 2,
        ),
        compiler_params=pltpu.CompilerParams(dimension_semantics=("arbitrary",)),
        interpret=interpret,
    )(*operands)


def block_bounds(doc_lengths_row, first_query, tok_rows):
    doc_ends = jnp.cumsum(doc_lengths_row).astype(jnp.int32)

    def doc_start(pos):
        return jnp.max(jnp.where(doc_ends <= pos, doc_ends, 0))

    diagonal = first_query // KEY_BLOCK
    lo_block = doc_start(first_query) // KEY_BLOCK
    full_block = (doc_start(first_query + tok_rows - 1) + KEY_BLOCK - 1) // KEY_BLOCK
    full_block = jnp.clip(full_block, lo_block, diagonal)
    hi_block = (first_query + tok_rows + KEY_BLOCK - 1) // KEY_BLOCK
    head = jnp.stack([first_query, lo_block, full_block, diagonal, hi_block]).astype(jnp.int32)
    return jnp.concatenate([head, doc_ends])


def local(queries, keys, values, doc_lengths, send_tile, take_slot):
    tok_rows = queries.shape[0]
    peer_count = lax.axis_size("cp")
    tile_rows = tok_rows // peer_count
    slot_count = send_tile.shape[1] // peer_count
    chosen = send_tile[0]
    placed = take_slot[0]

    def outgoing(source):
        tiled = source.reshape(peer_count, tile_rows, source.shape[1])
        picked = jnp.take(tiled, chosen, axis=0, mode="clip")
        return picked.reshape(peer_count * slot_count * tile_rows, source.shape[1])

    def incoming(source):
        tiled = source.reshape(peer_count * slot_count, tile_rows, source.shape[1])
        return jnp.take(tiled, placed, axis=0, mode="clip").reshape(tok_rows, source.shape[1])

    def relayout(source):
        sent = outgoing(source)
        return incoming(lax.all_to_all(sent, "cp", split_axis=0, concat_axis=0, tiled=True))

    own_kv = relayout(jnp.concatenate([keys, values], axis=1))
    all_kv = lax.all_gather(own_kv, "grp", axis=0, tiled=True)
    half = queries.shape[1] // 2
    first_queries = relayout(queries[:, :half])
    second_queries = relayout(queries[:, half:])
    member = lax.axis_index("grp")
    bounds = block_bounds(doc_lengths[0], member * tok_rows, tok_rows)
    half_heads = KEY_VALUE_HEADS // 2
    attended = attention(bounds, first_queries, all_kv, 0)
    return attention(bounds, second_queries, all_kv, half_heads, previous=attended)


def solution(mesh):
    return jax.shard_map(
        local,
        mesh=mesh,
        in_specs=(
            P(("cp", "grp"), None),
            P(("cp", "grp"), None),
            P(("cp", "grp"), None),
            P("cp", None),
            P(("cp", "grp"), None),
            P(("cp", "grp"), None),
        ),
        out_specs=P(("cp", "grp"), None),
        check_vma=False,
    )
```

```python
import functools
import math

import jax
import jax.numpy as jnp
from jax import lax
from jax.experimental import pallas as pl
from jax.experimental.pallas import tpu as pltpu
from jax.sharding import PartitionSpec as P

QUERY_HEADS = 64
KEY_VALUE_HEADS = 8
HEAD_SIZE = 128
KEY_BLOCK = 1024
LANES = 128
MASKED = -1e30


def attention_kernel(bounds, q_ref, k_ref, v_ref, *refs, previous=False):
    if previous:
        refs = refs[1:]
    o_ref, max_ref, total_ref, sum_ref = refs
    query_rows = q_ref.shape[0]
    queries_per_group = q_ref.shape[1] // HEAD_SIZE
    exp2_scale = math.log2(math.e) / math.sqrt(HEAD_SIZE)
    first_query = bounds[0]
    ends = [bounds[5], bounds[6], bounds[7]]

    query_pos = first_query + lax.broadcasted_iota(jnp.int32, (query_rows, 1), 0)
    query_start = jnp.zeros((query_rows, 1), jnp.int32)
    for end in ends:
        query_start = jnp.maximum(query_start, jnp.where(query_pos >= end, end, 0))

    max_ref[...] = jnp.full(max_ref.shape, MASKED, jnp.float32)
    total_ref[...] = jnp.zeros(total_ref.shape, jnp.float32)
    sum_ref[...] = jnp.zeros(sum_ref.shape, jnp.float32)

    def body(block, carry, masked):
        start = pl.multiple_of(block * KEY_BLOCK, KEY_BLOCK)
        key = k_ref[pl.ds(start, KEY_BLOCK), :]
        value = v_ref[pl.ds(start, KEY_BLOCK), :]
        if masked:
            key_pos = start + lax.broadcasted_iota(jnp.int32, (1, KEY_BLOCK), 1)
            allowed = (key_pos >= query_start) & (key_pos <= query_pos)
        for head in range(queries_per_group):
            query = q_ref[:, head * HEAD_SIZE:(head + 1) * HEAD_SIZE]
            scores = lax.dot_general(
                query, key, (((1,), (1,)), ((), ())), preferred_element_type=jnp.float32
            )
            if masked:
                scores = jnp.where(allowed, scores, MASKED)
            row_max = max_ref[head]
            block_max = jnp.max(scores, axis=1, keepdims=True) * exp2_scale
            new_max = jnp.maximum(row_max, block_max)
            rescale = jnp.exp2(row_max - new_max)
            weights = jnp.exp2(scores * exp2_scale - jnp.tile(new_max, (1, KEY_BLOCK // LANES)))
            total_ref[head] = rescale * total_ref[head] + jnp.sum(weights, axis=1, keepdims=True)
            sum_ref[head] = rescale * sum_ref[head] + jnp.dot(
                weights.astype(jnp.bfloat16), value, preferred_element_type=jnp.float32
            )
            max_ref[head] = new_max
        return carry

    masked_body = functools.partial(body, masked=True)
    lax.fori_loop(bounds[1], bounds[2], masked_body, 0)
    lax.fori_loop(bounds[2], bounds[3], functools.partial(body, masked=False), 0)
    lax.fori_loop(bounds[3], bounds[4], masked_body, 0)
    for head in range(queries_per_group):
        o_ref[:, head * HEAD_SIZE:(head + 1) * HEAD_SIZE] = (
            sum_ref[head] / total_ref[head]
        ).astype(o_ref.dtype)


def attention(bounds, own_queries, all_kv, head_offset, previous=None, interpret=False):
    tok_rows = own_queries.shape[0]
    group_length = all_kv.shape[0]
    kv_heads = all_kv.shape[1] // (2 * HEAD_SIZE)
    head_width = QUERY_HEADS // KEY_VALUE_HEADS * HEAD_SIZE
    call_heads = own_queries.shape[1] // head_width
    queries_per_group = head_width // HEAD_SIZE
    in_specs = [
        pl.BlockSpec((tok_rows, head_width), lambda h, b: (0, h)),
        pl.BlockSpec((group_length, HEAD_SIZE), lambda h, b: (0, h + head_offset)),
        pl.BlockSpec((group_length, HEAD_SIZE), lambda h, b: (0, h + head_offset + kv_heads)),
    ]
    operands = [bounds, own_queries, all_kv, all_kv]
    aliases = {}
    if previous is not None:
        in_specs.append(pl.BlockSpec(memory_space=pl.ANY))
        operands.append(previous)
        aliases = {4: 0}
    return pl.pallas_call(
        attention_kernel if previous is None else functools.partial(attention_kernel, previous=True),
        out_shape=jax.ShapeDtypeStruct((tok_rows, kv_heads * head_width), own_queries.dtype),
        grid_spec=pltpu.PrefetchScalarGridSpec(
            num_scalar_prefetch=1,
            grid=(call_heads,),
            in_specs=in_specs,
            out_specs=pl.BlockSpec((tok_rows, head_width), lambda h, b: (0, h + head_offset)),
            scratch_shapes=[
                pltpu.VMEM((queries_per_group, tok_rows, LANES), jnp.float32),
                pltpu.VMEM((queries_per_group, tok_rows, LANES), jnp.float32),
                pltpu.VMEM((queries_per_group, tok_rows, HEAD_SIZE), jnp.float32),
            ],
        ),
        input_output_aliases=aliases,
        cost_estimate=pl.CostEstimate(
            flops=4 * call_heads * queries_per_group * tok_rows * group_length * HEAD_SIZE,
            transcendentals=call_heads * queries_per_group * tok_rows * group_length,
            bytes_accessed=2 * own_queries.size * 2 + 2 * call_heads * group_length * HEAD_SIZE * 2,
        ),
        compiler_params=pltpu.CompilerParams(dimension_semantics=("arbitrary",)),
        interpret=interpret,
    )(*operands)


def block_bounds(doc_lengths_row, first_query, tok_rows):
    doc_ends = jnp.cumsum(doc_lengths_row).astype(jnp.int32)

    def doc_start(pos):
        return jnp.max(jnp.where(doc_ends <= pos, doc_ends, 0))

    diagonal = first_query // KEY_BLOCK
    lo_block = doc_start(first_query) // KEY_BLOCK
    full_block = (doc_start(first_query + tok_rows - 1) + KEY_BLOCK - 1) // KEY_BLOCK
    full_block = jnp.clip(full_block, lo_block, diagonal)
    hi_block = (first_query + tok_rows + KEY_BLOCK - 1) // KEY_BLOCK
    head = jnp.stack([first_query, lo_block, full_block, diagonal, hi_block]).astype(jnp.int32)
    return jnp.concatenate([head, doc_ends])


def local(queries, keys, values, doc_lengths, send_tile, take_slot):
    tok_rows = queries.shape[0]
    peer_count = lax.axis_size("cp")
    tile_rows = tok_rows // peer_count
    slot_count = send_tile.shape[1] // peer_count
    chosen = send_tile[0]
    placed = take_slot[0]

    def outgoing(source):
        tiled = source.reshape(peer_count, tile_rows, source.shape[1])
        picked = jnp.take(tiled, chosen, axis=0, mode="clip")
        return picked.reshape(peer_count * slot_count * tile_rows, source.shape[1])

    def incoming(source):
        tiled = source.reshape(peer_count * slot_count, tile_rows, source.shape[1])
        return jnp.take(tiled, placed, axis=0, mode="clip").reshape(tok_rows, source.shape[1])

    def relayout(source):
        sent = outgoing(source)
        return incoming(lax.all_to_all(sent, "cp", split_axis=0, concat_axis=0, tiled=True))

    own_kv = relayout(jnp.concatenate([keys, values], axis=1))
    all_kv = lax.all_gather(own_kv, "grp", axis=0, tiled=True)
    half = queries.shape[1] // 2
    first_queries = relayout(queries[:, :half])
    second_queries = relayout(queries[:, half:])
    member = lax.axis_index("grp")
    bounds = block_bounds(doc_lengths[0], member * tok_rows, tok_rows)
    half_heads = KEY_VALUE_HEADS // 2
    attended = attention(bounds, first_queries, all_kv, 0)
    return attention(bounds, second_queries, all_kv, half_heads, previous=attended)


def solution(mesh):
    return jax.shard_map(
        local,
        mesh=mesh,
        in_specs=(
            P(("cp", "grp"), None),
            P(("cp", "grp"), None),
            P(("cp", "grp"), None),
            P("cp", None),
            P(("cp", "grp"), None),
            P(("cp", "grp"), None),
        ),
        out_specs=P(("cp", "grp"), None),
        check_vma=False,
    )
```

```python
import functools
import math

import jax
import jax.numpy as jnp
from jax import lax
from jax.experimental import pallas as pl
from jax.experimental.pallas import tpu as pltpu
from jax.sharding import PartitionSpec as P

QUERY_HEADS = 64
KEY_VALUE_HEADS = 8
HEAD_SIZE = 128
KEY_BLOCK = 1024
LANES = 128
MASKED = -1e30


def attention_kernel(bounds, q_ref, k_ref, v_ref, *refs, previous=False):
    if previous:
        refs = refs[1:]
    o_ref, max_ref, total_ref, sum_ref = refs
    query_rows = q_ref.shape[0]
    queries_per_group = q_ref.shape[1] // HEAD_SIZE
    exp2_scale = math.log2(math.e) / math.sqrt(HEAD_SIZE)
    first_query = bounds[0]
    ends = [bounds[5], bounds[6], bounds[7]]

    query_pos = first_query + lax.broadcasted_iota(jnp.int32, (query_rows, 1), 0)
    query_start = jnp.zeros((query_rows, 1), jnp.int32)
    for end in ends:
        query_start = jnp.maximum(query_start, jnp.where(query_pos >= end, end, 0))

    max_ref[...] = jnp.full(max_ref.shape, MASKED, jnp.float32)
    total_ref[...] = jnp.zeros(total_ref.shape, jnp.float32)
    sum_ref[...] = jnp.zeros(sum_ref.shape, jnp.float32)

    def body(block, carry, masked):
        start = pl.multiple_of(block * KEY_BLOCK, KEY_BLOCK)
        key = k_ref[pl.ds(start, KEY_BLOCK), :]
        value = v_ref[pl.ds(start, KEY_BLOCK), :]
        if masked:
            key_pos = start + lax.broadcasted_iota(jnp.int32, (1, KEY_BLOCK), 1)
            allowed = (key_pos >= query_start) & (key_pos <= query_pos)
        for head in range(queries_per_group):
            query = q_ref[:, head * HEAD_SIZE:(head + 1) * HEAD_SIZE]
            scores = lax.dot_general(
                query, key, (((1,), (1,)), ((), ())), preferred_element_type=jnp.float32
            ) * exp2_scale
            if masked:
                scores = jnp.where(allowed, scores, MASKED)
            row_max = max_ref[head]
            new_max = jnp.maximum(row_max, jnp.max(scores, axis=1, keepdims=True))
            rescale = jnp.exp2(row_max - new_max)
            weights = jnp.exp2(scores - jnp.tile(new_max, (1, KEY_BLOCK // LANES)))
            total_ref[head] = rescale * total_ref[head] + jnp.sum(weights, axis=1, keepdims=True)
            sum_ref[head] = rescale * sum_ref[head] + jnp.dot(
                weights.astype(jnp.bfloat16), value, preferred_element_type=jnp.float32
            )
            max_ref[head] = new_max
        return carry

    masked_body = functools.partial(body, masked=True)
    lax.fori_loop(bounds[1], bounds[2], masked_body, 0)
    lax.fori_loop(bounds[2], bounds[3], functools.partial(body, masked=False), 0)
    lax.fori_loop(bounds[3], bounds[4], masked_body, 0)
    for head in range(queries_per_group):
        o_ref[:, head * HEAD_SIZE:(head + 1) * HEAD_SIZE] = (
            sum_ref[head] / total_ref[head]
        ).astype(o_ref.dtype)


def attention(bounds, own_queries, all_kv, head_offset, previous=None, interpret=False):
    tok_rows = own_queries.shape[0]
    group_length = all_kv.shape[0]
    kv_heads = all_kv.shape[1] // (2 * HEAD_SIZE)
    head_width = QUERY_HEADS // KEY_VALUE_HEADS * HEAD_SIZE
    call_heads = own_queries.shape[1] // head_width
    queries_per_group = head_width // HEAD_SIZE
    in_specs = [
        pl.BlockSpec((tok_rows, head_width), lambda h, b: (0, h)),
        pl.BlockSpec((group_length, HEAD_SIZE), lambda h, b: (0, h + head_offset)),
        pl.BlockSpec((group_length, HEAD_SIZE), lambda h, b: (0, h + head_offset + kv_heads)),
    ]
    operands = [bounds, own_queries, all_kv, all_kv]
    aliases = {}
    if previous is not None:
        in_specs.append(pl.BlockSpec(memory_space=pl.ANY))
        operands.append(previous)
        aliases = {4: 0}
    return pl.pallas_call(
        attention_kernel if previous is None else functools.partial(attention_kernel, previous=True),
        out_shape=jax.ShapeDtypeStruct((tok_rows, kv_heads * head_width), own_queries.dtype),
        grid_spec=pltpu.PrefetchScalarGridSpec(
            num_scalar_prefetch=1,
            grid=(call_heads,),
            in_specs=in_specs,
            out_specs=pl.BlockSpec((tok_rows, head_width), lambda h, b: (0, h + head_offset)),
            scratch_shapes=[
                pltpu.VMEM((queries_per_group, tok_rows, LANES), jnp.float32),
                pltpu.VMEM((queries_per_group, tok_rows, LANES), jnp.float32),
                pltpu.VMEM((queries_per_group, tok_rows, HEAD_SIZE), jnp.float32),
            ],
        ),
        input_output_aliases=aliases,
        cost_estimate=pl.CostEstimate(
            flops=4 * call_heads * queries_per_group * tok_rows * group_length * HEAD_SIZE,
            transcendentals=call_heads * queries_per_group * tok_rows * group_length,
            bytes_accessed=2 * own_queries.size * 2 + 2 * call_heads * group_length * HEAD_SIZE * 2,
        ),
        compiler_params=pltpu.CompilerParams(dimension_semantics=("arbitrary",)),
        interpret=interpret,
    )(*operands)


def block_bounds(doc_lengths_row, first_query, tok_rows):
    doc_ends = jnp.cumsum(doc_lengths_row).astype(jnp.int32)

    def doc_start(pos):
        return jnp.max(jnp.where(doc_ends <= pos, doc_ends, 0))

    diagonal = first_query // KEY_BLOCK
    lo_block = doc_start(first_query) // KEY_BLOCK
    full_block = (doc_start(first_query + tok_rows - 1) + KEY_BLOCK - 1) // KEY_BLOCK
    full_block = jnp.clip(full_block, lo_block, diagonal)
    hi_block = (first_query + tok_rows + KEY_BLOCK - 1) // KEY_BLOCK
    head = jnp.stack([first_query, lo_block, full_block, diagonal, hi_block]).astype(jnp.int32)
    return jnp.concatenate([head, doc_ends])


def local(queries, keys, values, doc_lengths, send_tile, take_slot):
    tok_rows = queries.shape[0]
    peer_count = lax.axis_size("cp")
    tile_rows = tok_rows // peer_count
    slot_count = send_tile.shape[1] // peer_count
    chosen = send_tile[0]
    placed = take_slot[0]

    def outgoing(source):
        tiled = source.reshape(peer_count, tile_rows, source.shape[1])
        picked = jnp.take(tiled, chosen, axis=0, mode="clip")
        return picked.reshape(peer_count * slot_count * tile_rows, source.shape[1])

    def incoming(source):
        tiled = source.reshape(peer_count * slot_count, tile_rows, source.shape[1])
        return jnp.take(tiled, placed, axis=0, mode="clip").reshape(tok_rows, source.shape[1])

    def relayout(source):
        sent = outgoing(source)
        return incoming(lax.all_to_all(sent, "cp", split_axis=0, concat_axis=0, tiled=True))

    own_kv = relayout(jnp.concatenate([keys, values], axis=1))
    all_kv = lax.all_gather(own_kv, "grp", axis=0, tiled=True)
    own_queries = relayout(queries)
    member = lax.axis_index("grp")
    bounds = block_bounds(doc_lengths[0], member * tok_rows, tok_rows)
    return attention(bounds, own_queries, all_kv, 0)


def solution(mesh):
    return jax.shard_map(
        local,
        mesh=mesh,
        in_specs=(
            P(("cp", "grp"), None),
            P(("cp", "grp"), None),
            P(("cp", "grp"), None),
            P("cp", None),
            P(("cp", "grp"), None),
            P(("cp", "grp"), None),
        ),
        out_specs=P(("cp", "grp"), None),
        check_vma=False,
    )
```

```python
import functools
import math

import jax
import jax.numpy as jnp
from jax import lax
from jax.experimental import pallas as pl
from jax.experimental.pallas import tpu as pltpu
from jax.sharding import PartitionSpec as P

QUERY_HEADS = 64
KEY_VALUE_HEADS = 8
HEAD_SIZE = 128
KEY_BLOCK = 1024
LANES = 128
MASKED = -1e30


def attention_kernel(bounds, q_ref, k_ref, v_ref, *refs, previous=False):
    if previous:
        refs = refs[1:]
    o_ref, max_ref, total_ref, sum_ref = refs
    query_rows = q_ref.shape[0]
    queries_per_group = q_ref.shape[1] // HEAD_SIZE
    exp2_scale = math.log2(math.e) / math.sqrt(HEAD_SIZE)
    first_query = bounds[0]
    ends = [bounds[5], bounds[6], bounds[7]]

    query_pos = first_query + lax.broadcasted_iota(jnp.int32, (query_rows, 1), 0)
    query_start = jnp.zeros((query_rows, 1), jnp.int32)
    for end in ends:
        query_start = jnp.maximum(query_start, jnp.where(query_pos >= end, end, 0))

    max_ref[...] = jnp.full(max_ref.shape, MASKED, jnp.float32)
    total_ref[...] = jnp.zeros(total_ref.shape, jnp.float32)
    sum_ref[...] = jnp.zeros(sum_ref.shape, jnp.float32)

    def body(block, carry, masked):
        start = pl.multiple_of(block * KEY_BLOCK, KEY_BLOCK)
        key = k_ref[pl.ds(start, KEY_BLOCK), :]
        value = v_ref[pl.ds(start, KEY_BLOCK), :]
        if masked:
            key_pos = start + lax.broadcasted_iota(jnp.int32, (1, KEY_BLOCK), 1)
            allowed = (key_pos >= query_start) & (key_pos <= query_pos)
        for head in range(queries_per_group):
            query = q_ref[:, head * HEAD_SIZE:(head + 1) * HEAD_SIZE]
            scores = lax.dot_general(
                query, key, (((1,), (1,)), ((), ())), preferred_element_type=jnp.float32
            ) * exp2_scale
            if masked:
                scores = jnp.where(allowed, scores, MASKED)
            row_max = max_ref[head]
            new_max = jnp.maximum(row_max, jnp.max(scores, axis=1, keepdims=True))
            rescale = jnp.exp2(row_max - new_max)
            weights = jnp.exp2(scores - jnp.tile(new_max, (1, KEY_BLOCK // LANES)))
            total_ref[head] = rescale * total_ref[head] + jnp.sum(weights, axis=1, keepdims=True)
            sum_ref[head] = rescale * sum_ref[head] + jnp.dot(
                weights.astype(jnp.bfloat16), value, preferred_element_type=jnp.float32
            )
            max_ref[head] = new_max
        return carry

    masked_body = functools.partial(body, masked=True)
    lax.fori_loop(bounds[1], bounds[2], masked_body, 0)
    lax.fori_loop(bounds[2], bounds[3], functools.partial(body, masked=False), 0)
    lax.fori_loop(bounds[3], bounds[4], masked_body, 0)
    for head in range(queries_per_group):
        o_ref[:, head * HEAD_SIZE:(head + 1) * HEAD_SIZE] = (
            sum_ref[head] / total_ref[head]
        ).astype(o_ref.dtype)


def attention(bounds, own_queries, all_kv, head_offset, previous=None, interpret=False):
    tok_rows = own_queries.shape[0]
    group_length = all_kv.shape[0]
    kv_heads = all_kv.shape[1] // (2 * HEAD_SIZE)
    head_width = QUERY_HEADS // KEY_VALUE_HEADS * HEAD_SIZE
    call_heads = own_queries.shape[1] // head_width
    queries_per_group = head_width // HEAD_SIZE
    in_specs = [
        pl.BlockSpec((tok_rows, head_width), lambda h, b: (0, h)),
        pl.BlockSpec((group_length, HEAD_SIZE), lambda h, b: (0, h + head_offset)),
        pl.BlockSpec((group_length, HEAD_SIZE), lambda h, b: (0, h + head_offset + kv_heads)),
    ]
    operands = [bounds, own_queries, all_kv, all_kv]
    aliases = {}
    if previous is not None:
        in_specs.append(pl.BlockSpec(memory_space=pl.ANY))
        operands.append(previous)
        aliases = {4: 0}
    return pl.pallas_call(
        attention_kernel if previous is None else functools.partial(attention_kernel, previous=True),
        out_shape=jax.ShapeDtypeStruct((tok_rows, kv_heads * head_width), own_queries.dtype),
        grid_spec=pltpu.PrefetchScalarGridSpec(
            num_scalar_prefetch=1,
            grid=(call_heads,),
            in_specs=in_specs,
            out_specs=pl.BlockSpec((tok_rows, head_width), lambda h, b: (0, h + head_offset)),
            scratch_shapes=[
                pltpu.VMEM((queries_per_group, tok_rows, LANES), jnp.float32),
                pltpu.VMEM((queries_per_group, tok_rows, LANES), jnp.float32),
                pltpu.VMEM((queries_per_group, tok_rows, HEAD_SIZE), jnp.float32),
            ],
        ),
        input_output_aliases=aliases,
        cost_estimate=pl.CostEstimate(
            flops=4 * call_heads * queries_per_group * tok_rows * group_length * HEAD_SIZE,
            transcendentals=call_heads * queries_per_group * tok_rows * group_length,
            bytes_accessed=2 * own_queries.size * 2 + 2 * call_heads * group_length * HEAD_SIZE * 2,
        ),
        compiler_params=pltpu.CompilerParams(dimension_semantics=("arbitrary",)),
        interpret=interpret,
    )(*operands)


def gathered_kernel(bounds, placed, got_hbm, k_ref, v_ref, o_ref, qbuf, sems, *state):
    step = pl.program_id(0)
    steps = pl.num_programs(0)
    tiles = placed.shape[0]
    tile_rows = qbuf.shape[1] // tiles
    width = qbuf.shape[2]
    slots_total = got_hbm.shape[0] // tile_rows

    def fetch(target_step, slot):
        for tile in range(tiles):
            source_slot = jnp.clip(placed[tile], 0, slots_total - 1)
            pltpu.make_async_copy(
                got_hbm.at[pl.ds(source_slot * tile_rows, tile_rows), pl.ds(target_step * width, width)],
                qbuf.at[slot, pl.ds(tile * tile_rows, tile_rows), :],
                sems.at[slot],
            ).start()

    @pl.when(step == 0)
    def _():
        fetch(0, 0)

    slot = step % 2

    @pl.when(step + 1 < steps)
    def _():
        fetch(step + 1, 1 - slot)

    pltpu.make_async_copy(
        got_hbm.at[pl.ds(0, qbuf.shape[1]), pl.ds(0, width)], qbuf.at[slot], sems.at[slot]
    ).wait()
    attention_kernel(bounds, qbuf.at[slot], k_ref, v_ref, o_ref, *state)


def attention_gathered(bounds, placed, got, all_kv, interpret=False):
    tok_rows = got.shape[0] // 2
    group_length = all_kv.shape[0]
    kv_heads = all_kv.shape[1] // (2 * HEAD_SIZE)
    head_width = got.shape[1] // kv_heads
    queries_per_group = head_width // HEAD_SIZE
    return pl.pallas_call(
        gathered_kernel,
        out_shape=jax.ShapeDtypeStruct((tok_rows, got.shape[1]), got.dtype),
        grid_spec=pltpu.PrefetchScalarGridSpec(
            num_scalar_prefetch=2,
            grid=(kv_heads,),
            in_specs=[
                pl.BlockSpec(memory_space=pl.ANY),
                pl.BlockSpec((group_length, HEAD_SIZE), lambda h, b, p: (0, h)),
                pl.BlockSpec((group_length, HEAD_SIZE), lambda h, b, p: (0, h + kv_heads)),
            ],
            out_specs=pl.BlockSpec((tok_rows, head_width), lambda h, b, p: (0, h)),
            scratch_shapes=[
                pltpu.VMEM((2, tok_rows, head_width), got.dtype),
                pltpu.SemaphoreType.DMA((2,)),
                pltpu.VMEM((queries_per_group, tok_rows, LANES), jnp.float32),
                pltpu.VMEM((queries_per_group, tok_rows, LANES), jnp.float32),
                pltpu.VMEM((queries_per_group, tok_rows, HEAD_SIZE), jnp.float32),
            ],
        ),
        cost_estimate=pl.CostEstimate(
            flops=4 * kv_heads * queries_per_group * tok_rows * group_length * HEAD_SIZE,
            transcendentals=kv_heads * queries_per_group * tok_rows * group_length,
            bytes_accessed=4 * tok_rows * got.shape[1] + 2 * kv_heads * group_length * HEAD_SIZE * 2,
        ),
        compiler_params=pltpu.CompilerParams(dimension_semantics=("arbitrary",)),
        interpret=interpret,
    )(bounds, placed, got, all_kv, all_kv)


def block_bounds(doc_lengths_row, first_query, tok_rows):
    doc_ends = jnp.cumsum(doc_lengths_row).astype(jnp.int32)

    def doc_start(pos):
        return jnp.max(jnp.where(doc_ends <= pos, doc_ends, 0))

    diagonal = first_query // KEY_BLOCK
    lo_block = doc_start(first_query) // KEY_BLOCK
    full_block = (doc_start(first_query + tok_rows - 1) + KEY_BLOCK - 1) // KEY_BLOCK
    full_block = jnp.clip(full_block, lo_block, diagonal)
    hi_block = (first_query + tok_rows + KEY_BLOCK - 1) // KEY_BLOCK
    head = jnp.stack([first_query, lo_block, full_block, diagonal, hi_block]).astype(jnp.int32)
    return jnp.concatenate([head, doc_ends])


def local(queries, keys, values, doc_lengths, send_tile, take_slot):
    tok_rows = queries.shape[0]
    peer_count = lax.axis_size("cp")
    tile_rows = tok_rows // peer_count
    slot_count = send_tile.shape[1] // peer_count
    chosen = send_tile[0]
    placed = take_slot[0]

    def outgoing(source):
        tiled = source.reshape(peer_count, tile_rows, source.shape[1])
        picked = jnp.take(tiled, chosen, axis=0, mode="clip")
        return picked.reshape(peer_count * slot_count * tile_rows, source.shape[1])

    def incoming(source):
        tiled = source.reshape(peer_count * slot_count, tile_rows, source.shape[1])
        return jnp.take(tiled, placed, axis=0, mode="clip").reshape(tok_rows, source.shape[1])

    def relayout(source):
        sent = outgoing(source)
        return incoming(lax.all_to_all(sent, "cp", split_axis=0, concat_axis=0, tiled=True))

    own_kv = relayout(jnp.concatenate([keys, values], axis=1))
    all_kv = lax.all_gather(own_kv, "grp", axis=0, tiled=True)
    got_queries = lax.all_to_all(outgoing(queries), "cp", split_axis=0, concat_axis=0, tiled=True)
    member = lax.axis_index("grp")
    bounds = block_bounds(doc_lengths[0], member * tok_rows, tok_rows)
    return attention_gathered(bounds, placed, got_queries, all_kv)


def solution(mesh):
    return jax.shard_map(
        local,
        mesh=mesh,
        in_specs=(
            P(("cp", "grp"), None),
            P(("cp", "grp"), None),
            P(("cp", "grp"), None),
            P("cp", None),
            P(("cp", "grp"), None),
            P(("cp", "grp"), None),
        ),
        out_specs=P(("cp", "grp"), None),
        check_vma=False,
    )
```

```python
import functools
import math

import jax
import jax.numpy as jnp
from jax import lax
from jax.experimental import pallas as pl
from jax.experimental.pallas import tpu as pltpu
from jax.sharding import PartitionSpec as P

QUERY_HEADS = 64
KEY_VALUE_HEADS = 8
HEAD_SIZE = 128
KEY_BLOCK = 1024
LANES = 128
MASKED = -1e30


def attention_kernel(bounds, q_ref, k_ref, v_ref, *refs, previous=False):
    if previous:
        refs = refs[1:]
    o_ref, max_ref, total_ref, sum_ref = refs
    query_rows = q_ref.shape[0]
    queries_per_group = q_ref.shape[1] // HEAD_SIZE
    exp2_scale = math.log2(math.e) / math.sqrt(HEAD_SIZE)
    first_query = bounds[0]
    ends = [bounds[5], bounds[6], bounds[7]]

    query_pos = first_query + lax.broadcasted_iota(jnp.int32, (query_rows, 1), 0)
    query_start = jnp.zeros((query_rows, 1), jnp.int32)
    for end in ends:
        query_start = jnp.maximum(query_start, jnp.where(query_pos >= end, end, 0))

    max_ref[...] = jnp.full(max_ref.shape, MASKED, jnp.float32)
    total_ref[...] = jnp.zeros(total_ref.shape, jnp.float32)
    sum_ref[...] = jnp.zeros(sum_ref.shape, jnp.float32)

    def body(block, carry, masked):
        start = pl.multiple_of(block * KEY_BLOCK, KEY_BLOCK)
        key = k_ref[pl.ds(start, KEY_BLOCK), :]
        value = v_ref[pl.ds(start, KEY_BLOCK), :]
        if masked:
            key_pos = start + lax.broadcasted_iota(jnp.int32, (1, KEY_BLOCK), 1)
            allowed = (key_pos >= query_start) & (key_pos <= query_pos)
        for head in range(queries_per_group):
            query = q_ref[:, head * HEAD_SIZE:(head + 1) * HEAD_SIZE]
            scores = lax.dot_general(
                query, key, (((1,), (1,)), ((), ())), preferred_element_type=jnp.float32
            ) * exp2_scale
            if masked:
                scores = jnp.where(allowed, scores, MASKED)
            row_max = max_ref[head]
            new_max = jnp.maximum(row_max, jnp.max(scores, axis=1, keepdims=True))
            rescale = jnp.exp2(row_max - new_max)
            weights = jnp.exp2(scores - jnp.tile(new_max, (1, KEY_BLOCK // LANES)))
            total_ref[head] = rescale * total_ref[head] + jnp.sum(weights, axis=1, keepdims=True)
            sum_ref[head] = rescale * sum_ref[head] + jnp.dot(
                weights.astype(jnp.bfloat16), value, preferred_element_type=jnp.float32
            )
            max_ref[head] = new_max
        return carry

    masked_body = functools.partial(body, masked=True)
    lax.fori_loop(bounds[1], bounds[2], masked_body, 0)
    lax.fori_loop(bounds[2], bounds[3], functools.partial(body, masked=False), 0)
    lax.fori_loop(bounds[3], bounds[4], masked_body, 0)
    for head in range(queries_per_group):
        o_ref[:, head * HEAD_SIZE:(head + 1) * HEAD_SIZE] = (
            sum_ref[head] / total_ref[head]
        ).astype(o_ref.dtype)


def attention(bounds, own_queries, all_kv, head_offset, previous=None, interpret=False):
    tok_rows = own_queries.shape[0]
    group_length = all_kv.shape[0]
    kv_heads = all_kv.shape[1] // (2 * HEAD_SIZE)
    head_width = QUERY_HEADS // KEY_VALUE_HEADS * HEAD_SIZE
    call_heads = own_queries.shape[1] // head_width
    queries_per_group = head_width // HEAD_SIZE
    in_specs = [
        pl.BlockSpec((tok_rows, head_width), lambda h, b: (0, h)),
        pl.BlockSpec((group_length, HEAD_SIZE), lambda h, b: (0, h + head_offset)),
        pl.BlockSpec((group_length, HEAD_SIZE), lambda h, b: (0, h + head_offset + kv_heads)),
    ]
    operands = [bounds, own_queries, all_kv, all_kv]
    aliases = {}
    if previous is not None:
        in_specs.append(pl.BlockSpec(memory_space=pl.ANY))
        operands.append(previous)
        aliases = {4: 0}
    return pl.pallas_call(
        attention_kernel if previous is None else functools.partial(attention_kernel, previous=True),
        out_shape=jax.ShapeDtypeStruct((tok_rows, kv_heads * head_width), own_queries.dtype),
        grid_spec=pltpu.PrefetchScalarGridSpec(
            num_scalar_prefetch=1,
            grid=(call_heads,),
            in_specs=in_specs,
            out_specs=pl.BlockSpec((tok_rows, head_width), lambda h, b: (0, h + head_offset)),
            scratch_shapes=[
                pltpu.VMEM((queries_per_group, tok_rows, LANES), jnp.float32),
                pltpu.VMEM((queries_per_group, tok_rows, LANES), jnp.float32),
                pltpu.VMEM((queries_per_group, tok_rows, HEAD_SIZE), jnp.float32),
            ],
        ),
        input_output_aliases=aliases,
        cost_estimate=pl.CostEstimate(
            flops=4 * call_heads * queries_per_group * tok_rows * group_length * HEAD_SIZE,
            transcendentals=call_heads * queries_per_group * tok_rows * group_length,
            bytes_accessed=2 * own_queries.size * 2 + 2 * call_heads * group_length * HEAD_SIZE * 2,
        ),
        compiler_params=pltpu.CompilerParams(dimension_semantics=("arbitrary",)),
        interpret=interpret,
    )(*operands)


def gathered_kernel(bounds, placed, got_hbm, k_ref, v_ref, o_ref, qbuf, sems, *state):
    step = pl.program_id(0)
    steps = pl.num_programs(0)
    tiles = placed.shape[0]
    tile_rows = qbuf.shape[1] // tiles
    width = qbuf.shape[2]
    slots_total = got_hbm.shape[0] // tile_rows

    def fetch(target_step, slot):
        for tile in range(tiles):
            source_slot = jnp.clip(placed[tile], 0, slots_total - 1)
            pltpu.make_async_copy(
                got_hbm.at[pl.ds(source_slot * tile_rows, tile_rows), pl.ds(target_step * width, width)],
                qbuf.at[slot, pl.ds(tile * tile_rows, tile_rows), :],
                sems.at[slot],
            ).start()

    @pl.when(step == 0)
    def _():
        fetch(0, 0)

    slot = step % 2

    @pl.when(step + 1 < steps)
    def _():
        fetch(step + 1, 1 - slot)

    pltpu.make_async_copy(
        got_hbm.at[pl.ds(0, qbuf.shape[1]), pl.ds(0, width)], qbuf.at[slot], sems.at[slot]
    ).wait()
    attention_kernel(bounds, qbuf.at[slot], k_ref, v_ref, o_ref, *state)


def attention_gathered(bounds, placed, got, all_kv, interpret=False):
    tok_rows = got.shape[0] // 2
    group_length = all_kv.shape[0]
    kv_heads = all_kv.shape[1] // (2 * HEAD_SIZE)
    head_width = got.shape[1] // kv_heads
    queries_per_group = head_width // HEAD_SIZE
    return pl.pallas_call(
        gathered_kernel,
        out_shape=jax.ShapeDtypeStruct((tok_rows, got.shape[1]), got.dtype),
        grid_spec=pltpu.PrefetchScalarGridSpec(
            num_scalar_prefetch=2,
            grid=(kv_heads,),
            in_specs=[
                pl.BlockSpec(memory_space=pl.ANY),
                pl.BlockSpec((group_length, HEAD_SIZE), lambda h, b, p: (0, h)),
                pl.BlockSpec((group_length, HEAD_SIZE), lambda h, b, p: (0, h + kv_heads)),
            ],
            out_specs=pl.BlockSpec((tok_rows, head_width), lambda h, b, p: (0, h)),
            scratch_shapes=[
                pltpu.VMEM((2, tok_rows, head_width), got.dtype),
                pltpu.SemaphoreType.DMA((2,)),
                pltpu.VMEM((queries_per_group, tok_rows, LANES), jnp.float32),
                pltpu.VMEM((queries_per_group, tok_rows, LANES), jnp.float32),
                pltpu.VMEM((queries_per_group, tok_rows, HEAD_SIZE), jnp.float32),
            ],
        ),
        cost_estimate=pl.CostEstimate(
            flops=4 * kv_heads * queries_per_group * tok_rows * group_length * HEAD_SIZE,
            transcendentals=kv_heads * queries_per_group * tok_rows * group_length,
            bytes_accessed=4 * tok_rows * got.shape[1] + 2 * kv_heads * group_length * HEAD_SIZE * 2,
        ),
        compiler_params=pltpu.CompilerParams(dimension_semantics=("arbitrary",)),
        interpret=interpret,
    )(bounds, placed, got, all_kv, all_kv)


def send_kernel(chosen, source_hbm, sent_hbm, sem):
    slots = chosen.shape[0]
    tile_rows = sent_hbm.shape[0] // slots
    tiles = source_hbm.shape[0] // tile_rows
    for slot in range(slots):
        tile = jnp.clip(chosen[slot], 0, tiles - 1)
        pltpu.make_async_copy(
            source_hbm.at[pl.ds(tile * tile_rows, tile_rows), :],
            sent_hbm.at[pl.ds(slot * tile_rows, tile_rows), :],
            sem.at[0],
        ).start()
    pltpu.make_async_copy(sent_hbm, sent_hbm, sem.at[0]).wait()


def send_buffer(chosen, source, interpret=False):
    tile_rows = source.shape[0] // (chosen.shape[0] // 2)
    return pl.pallas_call(
        send_kernel,
        out_shape=jax.ShapeDtypeStruct((chosen.shape[0] * tile_rows, source.shape[1]), source.dtype),
        grid_spec=pltpu.PrefetchScalarGridSpec(
            num_scalar_prefetch=1,
            grid=(),
            in_specs=[pl.BlockSpec(memory_space=pl.ANY)],
            out_specs=pl.BlockSpec(memory_space=pl.ANY),
            scratch_shapes=[pltpu.SemaphoreType.DMA((1,))],
        ),
        interpret=interpret,
    )(chosen, source)


def block_bounds(doc_lengths_row, first_query, tok_rows):
    doc_ends = jnp.cumsum(doc_lengths_row).astype(jnp.int32)

    def doc_start(pos):
        return jnp.max(jnp.where(doc_ends <= pos, doc_ends, 0))

    diagonal = first_query // KEY_BLOCK
    lo_block = doc_start(first_query) // KEY_BLOCK
    full_block = (doc_start(first_query + tok_rows - 1) + KEY_BLOCK - 1) // KEY_BLOCK
    full_block = jnp.clip(full_block, lo_block, diagonal)
    hi_block = (first_query + tok_rows + KEY_BLOCK - 1) // KEY_BLOCK
    head = jnp.stack([first_query, lo_block, full_block, diagonal, hi_block]).astype(jnp.int32)
    return jnp.concatenate([head, doc_ends])


def local(queries, keys, values, doc_lengths, send_tile, take_slot):
    tok_rows = queries.shape[0]
    peer_count = lax.axis_size("cp")
    tile_rows = tok_rows // peer_count
    slot_count = send_tile.shape[1] // peer_count
    chosen = send_tile[0]
    placed = take_slot[0]

    def outgoing(source):
        tiled = source.reshape(peer_count, tile_rows, source.shape[1])
        picked = jnp.take(tiled, chosen, axis=0, mode="clip")
        return picked.reshape(peer_count * slot_count * tile_rows, source.shape[1])

    def incoming(source):
        tiled = source.reshape(peer_count * slot_count, tile_rows, source.shape[1])
        return jnp.take(tiled, placed, axis=0, mode="clip").reshape(tok_rows, source.shape[1])

    def relayout(source):
        sent = outgoing(source)
        return incoming(lax.all_to_all(sent, "cp", split_axis=0, concat_axis=0, tiled=True))

    own_kv = relayout(jnp.concatenate([keys, values], axis=1))
    all_kv = lax.all_gather(own_kv, "grp", axis=0, tiled=True)
    got_queries = lax.all_to_all(
        send_buffer(chosen, queries), "cp", split_axis=0, concat_axis=0, tiled=True
    )
    member = lax.axis_index("grp")
    bounds = block_bounds(doc_lengths[0], member * tok_rows, tok_rows)
    return attention_gathered(bounds, placed, got_queries, all_kv)


def solution(mesh):
    return jax.shard_map(
        local,
        mesh=mesh,
        in_specs=(
            P(("cp", "grp"), None),
            P(("cp", "grp"), None),
            P(("cp", "grp"), None),
            P("cp", None),
            P(("cp", "grp"), None),
            P(("cp", "grp"), None),
        ),
        out_specs=P(("cp", "grp"), None),
        check_vma=False,
    )
```
